32 devices in a mesh: parts: 2 (over y), ctx: 8 (over z, x), tp: 2 (over core).
Axes of the slice: x: 2, y: 2, z: 4, core: 2. Of those that a mesh axis runs over, the one named last changes fastest.
Arguments:
- queries: bfloat16 [2048, 8192], P(('parts', 'ctx'), 'tp'), parts along dimension 0, may hold values from -9 to 9
- episode_key_cache: bfloat16 [128, 16, 1024], P(None, ('parts', 'ctx'), 'tp'), parts along dimension 1, may hold values from -9 to 9
- episode_value_cache: bfloat16 [128, 16, 1024], P(None, ('parts', 'ctx'), 'tp'), parts along dimension 1, may hold values from -6 to 6
- output_gradient: bfloat16 [2048, 8192], P(('parts', 'ctx'), 'tp'), parts along dimension 0, may hold values from -6 to 6
- block_lists: int32 [16, 2], P(('parts', 'ctx')), parts along dimension 0, may hold values from 0 to 7, as said below
- block_counts: int32 [16], P(('parts', 'ctx')), parts along dimension 0, may hold values from 1 to 2
Outputs:
- attn_out: bfloat16 [2048, 8192], P(('parts', 'ctx'), 'tp'), parts along dimension 0
- query_grad: bfloat16 [2048, 8192], P(('parts', 'ctx'), 'tp'), parts along dimension 0
- key_cache_gradient: bfloat16 [128, 16, 1024], P(None, ('parts', 'ctx'), 'tp'), parts along dimension 1
- value_cache_gradient: bfloat16 [128, 16, 1024], P(None, ('parts', 'ctx'), 'tp'), parts along dimension 1
The draws below stay inside these ranges and needn't reach their ends.
There are 2 independent parts, one for each index of `parts`. The reference program is written for one: setup_inputs(seed, part) draws one part's arguments, and reference() takes and returns one part's arrays. A program takes and returns all parts, laid end to end along the dimension named above; each array names one. Nothing has to cross between parts.
Inputs may be any that keep to these rules, and one draw needn't show every extreme that they name: `block_lists`: each row names 2 different key blocks; a query block reads only its first block_counts entries.
All inputs are finite; a program needn't handle non-finite values.
Results may differ from the reference program's by a relative error of at most 0.0085.
The reference program's roundings to bfloat16 on the way (of `weights_low` and `score_grad`) count: a program that leaves them out, or rounds other values in their place, can miss the bound.
Values may be sent and summed in bfloat16 or wider, within the bound.
No kernel may reach another device: no remote copies, remote signals or barrier semaphores. Data moves between devices by JAX's collectives and lax.ppermute only.
A program may use at most 64 MiB of HBM per device.

```python
import jax
import jax.numpy as jnp
from jax import lax

QUERY_HEADS = 64
KEY_VALUE_HEADS = 8
HEAD_SIZE = 128
BLOCK_TOKENS = 128
LIST = 2
QUERY_BLOCKS_NUM = 8
QTOK = 1024
KEY_BLOCK_COUNT = 8


def draw_queries(key, part):
    noise_random_seed = jax.random.fold_in(key, 1)
    drawn_blocks = jnp.clip(1.4 * jax.random.normal(noise_random_seed, (QTOK, QUERY_HEADS, HEAD_SIZE), jnp.float32), -8.0, 8.0)
    return drawn_blocks.reshape(QTOK, QUERY_HEADS * HEAD_SIZE).astype(jnp.bfloat16)


def draw_episode_key_cache(key, part):
    noise_random_seed = jax.random.fold_in(key, 3)
    drawn_blocks = jnp.clip(1.4 * jax.random.normal(noise_random_seed, (BLOCK_TOKENS, KEY_BLOCK_COUNT, KEY_VALUE_HEADS, HEAD_SIZE), jnp.float32), -8.0, 8.0)
    return drawn_blocks.reshape(BLOCK_TOKENS, KEY_BLOCK_COUNT, KEY_VALUE_HEADS * HEAD_SIZE).astype(jnp.bfloat16)


def draw_block_lists(key, part):
    block_position = jnp.arange(KEY_BLOCK_COUNT, dtype=jnp.int32)
    row_position = jnp.arange(QUERY_BLOCKS_NUM, dtype=jnp.int32)[:, None]
    block_priority = jax.random.randint(jax.random.fold_in(key, 5), (QUERY_BLOCKS_NUM, KEY_BLOCK_COUNT), 0, 65536)
    block_popularity = jax.random.randint(jax.random.fold_in(key, 6), (KEY_BLOCK_COUNT,), 0, 3) * 32768
    starting_row = jax.random.randint(jax.random.fold_in(key, 7), (), 0, QUERY_BLOCKS_NUM)
    ending_row = jax.random.randint(jax.random.fold_in(key, 8), (), 0, QUERY_BLOCKS_NUM)
    forced_extra_weight = jnp.where((row_position == starting_row) & (block_position[None, :] == KEY_BLOCK_COUNT - 1), 262144, 0)
    forced_extra_weight = forced_extra_weight + jnp.where((row_position == ending_row) & (block_position[None, :] == 0), 262144, 0)
    priority_sum_total = (block_priority + block_popularity[None, :] + forced_extra_weight) * KEY_BLOCK_COUNT + block_position[None, :]
    return lax.top_k(priority_sum_total, LIST)[1].astype(jnp.int32)


def draw_block_counts(key, part):
    count_draw = jax.random.randint(jax.random.fold_in(key, 9), (QUERY_BLOCKS_NUM,), 1, LIST + 1)
    fullest = jax.random.randint(jax.random.fold_in(key, 10), (), 0, QUERY_BLOCKS_NUM)
    return jnp.where(jnp.arange(QUERY_BLOCKS_NUM, dtype=jnp.int32) == fullest, LIST, count_draw).astype(jnp.int32)


def levels(key, shape, pieces, least, largest):
    factor_of, own = 1.0, jax.random.fold_in(key, 6)
    for axis_at, blocks in pieces:
        draws = jnp.exp(jax.random.uniform(jax.random.fold_in(own, axis_at), (blocks,), jnp.float32, least / len(pieces), largest / len(pieces)))
        factor_of = factor_of * jnp.repeat(draws, shape[axis_at] // blocks).reshape([-1 if axis == axis_at else 1 for axis in range(len(shape))])
    return factor_of


def scatter_about(stream_key, extent, scale, limit, cuts=(), held_as=jnp.bfloat16):
    entries = jax.random.normal(stream_key, extent, jnp.float32) * scale
    if len(cuts) > 0:
        entries = levels(stream_key, extent, cuts, -0.22, 0.18) * entries
    return jnp.clip(entries, min=-limit, max=limit).astype(held_as)


def setup_inputs(seed: int = 0, part: int = 0) -> dict:
    keys = jax.random.split(jax.random.key(seed), 7)
    part_splits = jax.random.split(jax.random.fold_in(keys[6], part), 7)
    return {
        "queries": draw_queries(jax.random.fold_in(jax.random.fold_in(keys[6], part), 71), part),
        "episode_key_cache": draw_episode_key_cache(jax.random.fold_in(jax.random.fold_in(keys[6], part), 71), part),
        "episode_value_cache": scatter_about(part_splits[2], (BLOCK_TOKENS, KEY_BLOCK_COUNT, KEY_VALUE_HEADS * HEAD_SIZE), 1.0, 6.0, ((1, 8), (2, 2))),
        "output_gradient": scatter_about(part_splits[3], (QTOK, QUERY_HEADS * HEAD_SIZE), 1.0, 6.0, ((0, 8), (1, 2))),
        "block_lists": draw_block_lists(jax.random.fold_in(jax.random.fold_in(keys[6], part), 71), part),
        "block_counts": draw_block_counts(jax.random.fold_in(jax.random.fold_in(keys[6], part), 71), part),
    }


def attend_group(query_part, key_part, value_part, grad_part, live_slots):
    score_scale = HEAD_SIZE ** -0.5
    query_wide = query_part.astype(jnp.float32)
    key_wide = key_part.astype(jnp.float32)
    value_wide = value_part.astype(jnp.float32)
    grad_wide = grad_part.astype(jnp.float32)
    scores = score_scale * jnp.einsum('qah,jkh->aqjk', query_wide, key_wide)
    masked = jnp.where(live_slots[None, None, :, None], scores, -jnp.inf)
    row_peak = jnp.max(masked, axis=(2, 3), keepdims=True)
    exponent = jnp.exp(masked - row_peak)
    weights = exponent / jnp.sum(exponent, axis=(2, 3), keepdims=True)
    weights_low = weights.astype(jnp.bfloat16)
    attended = jnp.einsum('aqjk,jkh->qah', weights_low.astype(jnp.float32), value_wide).astype(jnp.bfloat16)
    attended = lax.optimization_barrier(attended)
    row_delta = jnp.sum(grad_wide * attended.astype(jnp.float32), axis=2)
    weight_grad = jnp.einsum('qah,jkh->aqjk', grad_wide, value_wide)
    score_grad = (weights * (weight_grad - row_delta.T[:, :, None, None])).astype(jnp.bfloat16)
    score_wide = score_grad.astype(jnp.float32)
    query_grad = (score_scale * jnp.einsum('aqjk,jkh->qah', score_wide, key_wide)).astype(jnp.bfloat16)
    key_piece = score_scale * jnp.einsum('aqjk,qah->jkh', score_wide, query_wide)
    value_piece = jnp.einsum('aqjk,qah->jkh', weights_low.astype(jnp.float32), grad_wide)
    return attended, query_grad, key_piece, value_piece


def reference(queries, episode_key_cache, episode_value_cache, output_gradient, block_lists, block_counts):
    queries_per_group = QUERY_HEADS // KEY_VALUE_HEADS
    query_block_list = queries.reshape(QUERY_BLOCKS_NUM, BLOCK_TOKENS, KEY_VALUE_HEADS, queries_per_group, HEAD_SIZE)
    gradient_blocks = output_gradient.reshape(QUERY_BLOCKS_NUM, BLOCK_TOKENS, KEY_VALUE_HEADS, queries_per_group, HEAD_SIZE)
    key_block_list = jnp.transpose(episode_key_cache, (1, 0, 2)).reshape(KEY_BLOCK_COUNT, BLOCK_TOKENS, KEY_VALUE_HEADS, HEAD_SIZE)
    value_block_list = jnp.transpose(episode_value_cache, (1, 0, 2)).reshape(KEY_BLOCK_COUNT, BLOCK_TOKENS, KEY_VALUE_HEADS, HEAD_SIZE)
    grouped = jax.vmap(attend_group, in_axes=(1, 2, 2, 1, None), out_axes=(1, 1, 2, 2))

    def one_block(carry, inputs):
        key_total, value_total = carry
        query_block, grad_block, listed, count = inputs
        live_slots = jnp.arange(LIST, dtype=jnp.int32) < count
        picked_keys = jnp.take(key_block_list, listed, axis=0)
        picked_values = jnp.take(value_block_list, listed, axis=0)
        attended, query_grad, key_piece, value_piece = grouped(query_block, picked_keys, picked_values, grad_block, live_slots)
        key_total = key_total.at[listed].add(key_piece)
        value_total = value_total.at[listed].add(value_piece)
        return (key_total, value_total), (attended, query_grad)

    start_offset = jnp.zeros((KEY_BLOCK_COUNT, BLOCK_TOKENS, KEY_VALUE_HEADS, HEAD_SIZE), jnp.float32)
    total_sums, stacked = lax.scan(one_block, (start_offset, start_offset), (query_block_list, gradient_blocks, block_lists, block_counts))
    attn_out = stacked[0].reshape(QTOK, QUERY_HEADS * HEAD_SIZE)
    query_grad = stacked[1].reshape(QTOK, QUERY_HEADS * HEAD_SIZE)
    key_cache_gradient = jnp.transpose(total_sums[0].reshape(KEY_BLOCK_COUNT, BLOCK_TOKENS, KEY_VALUE_HEADS * HEAD_SIZE), (1, 0, 2)).astype(jnp.bfloat16)
    value_cache_gradient = jnp.transpose(total_sums[1].reshape(KEY_BLOCK_COUNT, BLOCK_TOKENS, KEY_VALUE_HEADS * HEAD_SIZE), (1, 0, 2)).astype(jnp.bfloat16)
    return attn_out, query_grad, key_cache_gradient, value_cache_gradient
```

```python
import jax
import jax.numpy as jnp
from jax import lax
from jax.sharding import PartitionSpec as P

QUERY_HEADS = 64
KEY_VALUE_HEADS = 8
HEAD_SIZE = 128
LIST = 2
TAG_COLUMNS = 128


def attend(query_part, key_part, value_part, grad_part, live_slots):
    score_scale = HEAD_SIZE ** (-0.5)
    scores = score_scale * jnp.einsum(
        "qgah,jkgh->gaqjk", query_part, key_part, preferred_element_type=jnp.float32
    )
    masked = jnp.where(live_slots[None, None, None, :, None], scores, -jnp.inf)
    row_peak = jnp.max(masked, axis=(3, 4), keepdims=True)
    exponent = jnp.exp(masked - row_peak)
    weights = exponent / jnp.sum(exponent, axis=(3, 4), keepdims=True)
    weights_low = weights.astype(jnp.bfloat16)
    attended = jnp.einsum(
        "gaqjk,jkgh->qgah", weights_low, value_part, preferred_element_type=jnp.float32
    ).astype(jnp.bfloat16)
    attended = lax.optimization_barrier(attended)
    row_delta = jnp.sum(grad_part.astype(jnp.float32) * attended.astype(jnp.float32), axis=3)
    weight_grad = jnp.einsum(
        "qgah,jkgh->gaqjk", grad_part, value_part, preferred_element_type=jnp.float32
    )
    score_grad = (
        weights * (weight_grad - jnp.transpose(row_delta, (1, 2, 0))[:, :, :, None, None])
    ).astype(jnp.bfloat16)
    query_grad = (
        score_scale
        * jnp.einsum("gaqjk,jkgh->qgah", score_grad, key_part, preferred_element_type=jnp.float32)
    ).astype(jnp.bfloat16)
    key_piece = score_scale * jnp.einsum(
        "gaqjk,qgah->jkgh", score_grad, query_part, preferred_element_type=jnp.float32
    )
    value_piece = jnp.einsum(
        "gaqjk,qgah->jkgh", weights_low, grad_part, preferred_element_type=jnp.float32
    )
    return attended, query_grad, key_piece, value_piece


def make_shards(peers):
    def shards(
        queries, episode_key_cache, episode_value_cache, output_gradient, block_lists, block_counts
    ):
        row_count = episode_key_cache.shape[0]
        key_width = episode_key_cache.shape[2]
        both_width = 2 * key_width
        chunk_rows = row_count // peers
        local_groups = key_width // HEAD_SIZE
        queries_per_group = QUERY_HEADS // KEY_VALUE_HEADS
        query_rows = queries.shape[0]

        held = jnp.concatenate(
            [episode_key_cache[:, 0, :], episode_value_cache[:, 0, :]], axis=1
        )
        tag = jnp.concatenate([block_lists[0], block_counts]).astype(jnp.bfloat16)
        tag_block = jnp.zeros((row_count, TAG_COLUMNS), jnp.bfloat16)
        tag_block = tag_block.at[:, : LIST + 1].set(jnp.broadcast_to(tag, (row_count, LIST + 1)))
        first_send = jnp.concatenate([held, tag_block], axis=1).reshape(
            peers, chunk_rows, both_width + TAG_COLUMNS
        )
        first_recv = lax.all_to_all(first_send, "ctx", 0, 0, tiled=True)
        info = first_recv[:, 0, both_width : both_width + LIST + 1].astype(jnp.int32)
        lists_all = info[:, :LIST]
        counts_all = info[:, LIST]

        rows_held = first_recv[:, :, :both_width]
        picked = jnp.take(rows_held, lists_all, axis=0, mode="clip")
        fetched = lax.all_to_all(picked, "ctx", 0, 2, tiled=True)[0]
        key_rows = fetched[:, :, :key_width].reshape(LIST, row_count, local_groups, HEAD_SIZE)
        value_rows = fetched[:, :, key_width:].reshape(LIST, row_count, local_groups, HEAD_SIZE)

        live_slots = jnp.arange(LIST, dtype=jnp.int32) < block_counts[0]
        query_part = queries.reshape(query_rows, local_groups, queries_per_group, HEAD_SIZE)
        grad_part = output_gradient.reshape(query_rows, local_groups, queries_per_group, HEAD_SIZE)
        attended, query_grad, key_piece, value_piece = attend(
            query_part, key_rows, value_rows, grad_part, live_slots
        )

        pieces = jnp.concatenate(
            [
                key_piece.reshape(LIST, row_count, key_width),
                value_piece.reshape(LIST, row_count, key_width),
            ],
            axis=2,
        ).astype(jnp.bfloat16)
        back = lax.all_to_all(
            pieces.reshape(LIST, peers, chunk_rows, both_width), "ctx", 1, 1, tiled=True
        )
        slot_live = jnp.arange(LIST, dtype=jnp.int32)[None, :] < counts_all[:, None]
        selector = (
            (lists_all[:, :, None] == jnp.arange(peers, dtype=jnp.int32)[None, None, :])
            & slot_live[:, :, None]
        ).astype(jnp.bfloat16)
        summed = jnp.einsum(
            "jqrc,qjn->nrc", back, selector, preferred_element_type=jnp.float32
        ).astype(jnp.bfloat16)

        owned = lax.all_to_all(summed, "ctx", 0, 0, tiled=True).reshape(row_count, both_width)
        key_cache_gradient = owned[:, None, :key_width]
        value_cache_gradient = owned[:, None, key_width:]
        attn_out = attended.reshape(query_rows, local_groups * queries_per_group * HEAD_SIZE)
        query_grad = query_grad.reshape(query_rows, local_groups * queries_per_group * HEAD_SIZE)
        return attn_out, query_grad, key_cache_gradient, value_cache_gradient

    return shards


def solution(mesh):
    placed = (
        P(("parts", "ctx"), "tp"),
        P(None, ("parts", "ctx"), "tp"),
        P(None, ("parts", "ctx"), "tp"),
        P(("parts", "ctx"), "tp"),
        P(("parts", "ctx"), None),
        P(("parts", "ctx")),
    )
    return jax.shard_map(
        make_shards(mesh.shape["ctx"]),
        mesh=mesh,
        in_specs=placed,
        out_specs=(
            P(("parts", "ctx"), "tp"),
            P(("parts", "ctx"), "tp"),
            P(None, ("parts", "ctx"), "tp"),
            P(None, ("parts", "ctx"), "tp"),
        ),
        check_vma=False,
    )
```

```python
import jax
import jax.numpy as jnp
from jax import lax
from jax.experimental import pallas as pl
from jax.experimental.pallas import tpu as pltpu
from jax.sharding import PartitionSpec as P

QUERY_HEADS = 64
KEY_VALUE_HEADS = 8
HEAD_SIZE = 128
LIST = 2
TAG_COLUMNS = 128


def attention_kernel(chunk_rows, heads_per_group):
    score_scale = HEAD_SIZE ** (-0.5)

    def kernel(count_ref, q_ref, do_ref, k_ref, v_ref, o_ref, dq_ref, dk_ref, dv_ref):
        keys = k_ref[...]
        values = v_ref[...]
        key_total = keys.shape[0]
        slot = (lax.broadcasted_iota(jnp.int32, (1, key_total), 1) // chunk_rows) % LIST
        live = slot < count_ref[0]
        nt = (((1,), (1,)), ((), ()))
        tn = (((0,), (0,)), ((), ()))
        key_acc = jnp.zeros((key_total, HEAD_SIZE), jnp.float32)
        value_acc = jnp.zeros((key_total, HEAD_SIZE), jnp.float32)
        for head in range(heads_per_group):
            cols = slice(head * HEAD_SIZE, (head + 1) * HEAD_SIZE)
            q = q_ref[:, cols]
            do = do_ref[:, cols]
            scores = score_scale * lax.dot_general(
                q, keys, nt, preferred_element_type=jnp.float32
            )
            masked = jnp.where(live, scores, -jnp.inf)
            peak = jnp.max(masked, axis=1, keepdims=True)
            exponent = jnp.exp(masked - peak)
            weights = exponent / jnp.sum(exponent, axis=1, keepdims=True)
            weights_low = weights.astype(jnp.bfloat16)
            attended = jnp.dot(
                weights_low, values, preferred_element_type=jnp.float32
            ).astype(jnp.bfloat16)
            o_ref[:, cols] = attended
            row_delta = jnp.sum(
                do.astype(jnp.float32) * attended.astype(jnp.float32), axis=1, keepdims=True
            )
            weight_grad = lax.dot_general(do, values, nt, preferred_element_type=jnp.float32)
            score_grad = (weights * (weight_grad - row_delta)).astype(jnp.bfloat16)
            dq_ref[:, cols] = (
                score_scale * jnp.dot(score_grad, keys, preferred_element_type=jnp.float32)
            ).astype(jnp.bfloat16)
            key_acc = key_acc + lax.dot_general(
                score_grad, q, tn, preferred_element_type=jnp.float32
            )
            value_acc = value_acc + lax.dot_general(
                weights_low, do, tn, preferred_element_type=jnp.float32
            )
        dk_ref[...] = (score_scale * key_acc).astype(jnp.bfloat16)
        dv_ref[...] = value_acc.astype(jnp.bfloat16)

    return kernel


def attend_all(queries, output_gradient, fetched, count, chunk_rows):
    query_rows, query_width = queries.shape
    key_total, both_width = fetched.shape
    key_width = both_width // 2
    local_groups = key_width // HEAD_SIZE
    heads_per_group = QUERY_HEADS // KEY_VALUE_HEADS
    group_width = heads_per_group * HEAD_SIZE
    row_block = pl.BlockSpec((query_rows, group_width), lambda g: (0, g))
    key_block = pl.BlockSpec((key_total, HEAD_SIZE), lambda g: (0, g))
    value_block = pl.BlockSpec((key_total, HEAD_SIZE), lambda g: (0, local_groups + g))
    return pl.pallas_call(
        attention_kernel(chunk_rows, heads_per_group),
        grid=(local_groups,),
        in_specs=[
            pl.BlockSpec(memory_space=pltpu.SMEM),
            row_block,
            row_block,
            key_block,
            value_block,
        ],
        out_specs=[row_block, row_block, key_block, key_block],
        out_shape=[
            jax.ShapeDtypeStruct((query_rows, query_width), jnp.bfloat16),
            jax.ShapeDtypeStruct((query_rows, query_width), jnp.bfloat16),
            jax.ShapeDtypeStruct((key_total, key_width), jnp.bfloat16),
            jax.ShapeDtypeStruct((key_total, key_width), jnp.bfloat16),
        ],
    )(count, queries, output_gradient, fetched, fetched)


def make_shards(peers):
    def shards(
        queries, episode_key_cache, episode_value_cache, output_gradient, block_lists, block_counts
    ):
        row_count = episode_key_cache.shape[0]
        key_width = episode_key_cache.shape[2]
        both_width = 2 * key_width
        chunk_rows = row_count // peers

        held = jnp.concatenate(
            [episode_key_cache[:, 0, :], episode_value_cache[:, 0, :]], axis=1
        )
        tag = jnp.concatenate([block_lists[0], block_counts]).astype(jnp.bfloat16)
        tag_block = jnp.zeros((row_count, TAG_COLUMNS), jnp.bfloat16)
        tag_block = tag_block.at[:, : LIST + 1].set(jnp.broadcast_to(tag, (row_count, LIST + 1)))
        first_send = jnp.concatenate([held, tag_block], axis=1).reshape(
            peers, chunk_rows, both_width + TAG_COLUMNS
        )
        first_recv = lax.all_to_all(first_send, "ctx", 0, 0, tiled=True)
        info = first_recv[:, 0, both_width : both_width + LIST + 1].astype(jnp.int32)
        lists_all = info[:, :LIST]
        counts_all = info[:, LIST]

        rows_held = first_recv[:, :, :both_width]
        picked = jnp.take(rows_held, lists_all, axis=0, mode="clip")
        fetched = lax.all_to_all(picked, "ctx", 0, 0, tiled=True).reshape(
            LIST * row_count, both_width
        )
        attn_out, query_grad, key_piece, value_piece = attend_all(
            queries,
            output_gradient,
            fetched,
            block_counts,
            chunk_rows,
        )

        pieces = jnp.concatenate([key_piece, value_piece], axis=1).reshape(
            peers, LIST, chunk_rows, both_width
        )
        back = lax.all_to_all(pieces, "ctx", 0, 0, tiled=True)
        slot_live = jnp.arange(LIST, dtype=jnp.int32)[None, :] < counts_all[:, None]
        selector = (
            (lists_all[:, :, None] == jnp.arange(peers, dtype=jnp.int32)[None, None, :])
            & slot_live[:, :, None]
        ).astype(jnp.bfloat16)
        summed = jnp.einsum(
            "qjrc,qjn->nrc", back, selector, preferred_element_type=jnp.float32
        ).astype(jnp.bfloat16)

        owned = lax.all_to_all(summed, "ctx", 0, 0, tiled=True).reshape(row_count, both_width)
        key_cache_gradient = owned[:, None, :key_width]
        value_cache_gradient = owned[:, None, key_width:]
        return attn_out, query_grad, key_cache_gradient, value_cache_gradient

    return shards


def solution(mesh):
    placed = (
        P(("parts", "ctx"), "tp"),
        P(None, ("parts", "ctx"), "tp"),
        P(None, ("parts", "ctx"), "tp"),
        P(("parts", "ctx"), "tp"),
        P(("parts", "ctx"), None),
        P(("parts", "ctx")),
    )
    return jax.shard_map(
        make_shards(mesh.shape["ctx"]),
        mesh=mesh,
        in_specs=placed,
        out_specs=(
            P(("parts", "ctx"), "tp"),
            P(("parts", "ctx"), "tp"),
            P(None, ("parts", "ctx"), "tp"),
            P(None, ("parts", "ctx"), "tp"),
        ),
        check_vma=False,
    )
```

```python
import jax
import jax.numpy as jnp
from jax import lax
from jax.experimental import pallas as pl
from jax.experimental.pallas import tpu as pltpu
from jax.sharding import PartitionSpec as P

QUERY_HEADS = 64
KEY_VALUE_HEADS = 8
HEAD_SIZE = 128
LIST = 2
TAG_COLUMNS = 128


def attention_kernel(chunk_rows, heads_per_group):
    score_scale = HEAD_SIZE ** (-0.5)

    def kernel(count_ref, q_ref, do_ref, k_ref, v_ref, o_ref, dq_ref, dk_ref, dv_ref):
        keys = k_ref[...]
        values = v_ref[...]
        key_total = keys.shape[0]
        query_rows = q_ref.shape[0]
        slot = (lax.broadcasted_iota(jnp.int32, (1, key_total), 1) // chunk_rows) % LIST
        live = slot < count_ref[0]
        nt = (((1,), (1,)), ((), ()))
        tn = (((0,), (0,)), ((), ()))
        heads = [slice(a * HEAD_SIZE, (a + 1) * HEAD_SIZE) for a in range(heads_per_group)]
        q = jnp.concatenate([q_ref[:, cols] for cols in heads], axis=0)
        do = jnp.concatenate([do_ref[:, cols] for cols in heads], axis=0)
        scores = score_scale * lax.dot_general(q, keys, nt, preferred_element_type=jnp.float32)
        masked = jnp.where(live, scores, -jnp.inf)
        peak = jnp.max(masked, axis=1, keepdims=True)
        exponent = jnp.exp(masked - peak)
        weights = exponent / jnp.sum(exponent, axis=1, keepdims=True)
        weights_low = weights.astype(jnp.bfloat16)
        attended = jnp.dot(weights_low, values, preferred_element_type=jnp.float32).astype(
            jnp.bfloat16
        )
        row_delta = jnp.sum(
            do.astype(jnp.float32) * attended.astype(jnp.float32), axis=1, keepdims=True
        )
        weight_grad = lax.dot_general(do, values, nt, preferred_element_type=jnp.float32)
        score_grad = (weights * (weight_grad - row_delta)).astype(jnp.bfloat16)
        query_grad = (
            score_scale * jnp.dot(score_grad, keys, preferred_element_type=jnp.float32)
        ).astype(jnp.bfloat16)
        for a, cols in enumerate(heads):
            o_ref[:, cols] = attended[a * query_rows : (a + 1) * query_rows]
            dq_ref[:, cols] = query_grad[a * query_rows : (a + 1) * query_rows]
        dk_ref[...] = (
            score_scale * lax.dot_general(score_grad, q, tn, preferred_element_type=jnp.float32)
        ).astype(jnp.bfloat16)
        dv_ref[...] = lax.dot_general(
            weights_low, do, tn, preferred_element_type=jnp.float32
        ).astype(jnp.bfloat16)

    return kernel


def attend_all(queries, output_gradient, fetched, count, chunk_rows):
    query_rows, query_width = queries.shape
    key_total, both_width = fetched.shape
    key_width = both_width // 2
    local_groups = key_width // HEAD_SIZE
    heads_per_group = QUERY_HEADS // KEY_VALUE_HEADS
    group_width = heads_per_group * HEAD_SIZE
    row_block = pl.BlockSpec((query_rows, group_width), lambda g: (0, g))
    key_block = pl.BlockSpec((key_total, HEAD_SIZE), lambda g: (0, g))
    value_block = pl.BlockSpec((key_total, HEAD_SIZE), lambda g: (0, local_groups + g))
    return pl.pallas_call(
        attention_kernel(chunk_rows, heads_per_group),
        grid=(local_groups,),
        in_specs=[
            pl.BlockSpec(memory_space=pltpu.SMEM),
            row_block,
            row_block,
            key_block,
            value_block,
        ],
        out_specs=[row_block, row_block, key_block, key_block],
        out_shape=[
            jax.ShapeDtypeStruct((query_rows, query_width), jnp.bfloat16),
            jax.ShapeDtypeStruct((query_rows, query_width), jnp.bfloat16),
            jax.ShapeDtypeStruct((key_total, key_width), jnp.bfloat16),
            jax.ShapeDtypeStruct((key_total, key_width), jnp.bfloat16),
        ],
    )(count, queries, output_gradient, fetched, fetched)


def make_shards(peers):
    def shards(
        queries, episode_key_cache, episode_value_cache, output_gradient, block_lists, block_counts
    ):
        row_count = episode_key_cache.shape[0]
        key_width = episode_key_cache.shape[2]
        both_width = 2 * key_width
        chunk_rows = row_count // peers

        held = jnp.concatenate(
            [episode_key_cache[:, 0, :], episode_value_cache[:, 0, :]], axis=1
        )
        tag = jnp.concatenate([block_lists[0], block_counts]).astype(jnp.bfloat16)
        tag_block = jnp.zeros((row_count, TAG_COLUMNS), jnp.bfloat16)
        tag_block = tag_block.at[:, : LIST + 1].set(jnp.broadcast_to(tag, (row_count, LIST + 1)))
        first_send = jnp.concatenate([held, tag_block], axis=1).reshape(
            peers, chunk_rows, both_width + TAG_COLUMNS
        )
        first_recv = lax.all_to_all(first_send, "ctx", 0, 0, tiled=True)
        info = first_recv[:, 0, both_width : both_width + LIST + 1].astype(jnp.int32)
        lists_all = info[:, :LIST]
        counts_all = info[:, LIST]

        rows_held = first_recv[:, :, :both_width]
        picked = jnp.take(rows_held, lists_all, axis=0, mode="clip")
        fetched = lax.all_to_all(picked, "ctx", 0, 0, tiled=True).reshape(
            LIST * row_count, both_width
        )
        attn_out, query_grad, key_piece, value_piece = attend_all(
            queries,
            output_gradient,
            fetched,
            block_counts,
            chunk_rows,
        )

        pieces = jnp.concatenate([key_piece, value_piece], axis=1).reshape(
            peers, LIST, chunk_rows, both_width
        )
        back = lax.all_to_all(pieces, "ctx", 0, 0, tiled=True)
        slot_live = jnp.arange(LIST, dtype=jnp.int32)[None, :] < counts_all[:, None]
        selector = (
            (lists_all[:, :, None] == jnp.arange(peers, dtype=jnp.int32)[None, None, :])
            & slot_live[:, :, None]
        ).astype(jnp.bfloat16)
        summed = jnp.einsum(
            "qjrc,qjn->nrc", back, selector, preferred_element_type=jnp.float32
        ).astype(jnp.bfloat16)

        owned = lax.all_to_all(summed, "ctx", 0, 0, tiled=True).reshape(row_count, both_width)
        key_cache_gradient = owned[:, None, :key_width]
        value_cache_gradient = owned[:, None, key_width:]
        return attn_out, query_grad, key_cache_gradient, value_cache_gradient

    return shards


def solution(mesh):
    placed = (
        P(("parts", "ctx"), "tp"),
        P(None, ("parts", "ctx"), "tp"),
        P(None, ("parts", "ctx"), "tp"),
        P(("parts", "ctx"), "tp"),
        P(("parts", "ctx"), None),
        P(("parts", "ctx")),
    )
    return jax.shard_map(
        make_shards(mesh.shape["ctx"]),
        mesh=mesh,
        in_specs=placed,
        out_specs=(
            P(("parts", "ctx"), "tp"),
            P(("parts", "ctx"), "tp"),
            P(None, ("parts", "ctx"), "tp"),
            P(None, ("parts", "ctx"), "tp"),
        ),
        check_vma=False,
    )
```

```python
import jax
import jax.numpy as jnp
from jax import lax
from jax.experimental import pallas as pl
from jax.experimental.pallas import tpu as pltpu
from jax.sharding import PartitionSpec as P

QUERY_HEADS = 64
KEY_VALUE_HEADS = 8
HEAD_SIZE = 128
LIST = 2
TAG_COLUMNS = 128


def attention_kernel(chunk_rows, heads_per_group, local_groups):
    score_scale = HEAD_SIZE ** (-0.5)

    def kernel(count_ref, q_ref, do_ref, k_ref, v_ref, o_ref, dq_ref, pieces_ref):
        keys = k_ref[...]
        values = v_ref[...]
        key_total = keys.shape[0]
        query_rows = q_ref.shape[0]
        slot = (lax.broadcasted_iota(jnp.int32, (1, key_total), 1) // chunk_rows) % LIST
        live = slot < count_ref[0]
        nt = (((1,), (1,)), ((), ()))
        tn = (((0,), (0,)), ((), ()))
        heads = [slice(a * HEAD_SIZE, (a + 1) * HEAD_SIZE) for a in range(heads_per_group)]
        q = jnp.concatenate([q_ref[:, cols] for cols in heads], axis=0)
        do = jnp.concatenate([do_ref[:, cols] for cols in heads], axis=0)
        scores = score_scale * lax.dot_general(q, keys, nt, preferred_element_type=jnp.float32)
        masked = jnp.where(live, scores, -jnp.inf)
        peak = jnp.max(masked, axis=1, keepdims=True)
        exponent = jnp.exp(masked - peak)
        weights = exponent / jnp.sum(exponent, axis=1, keepdims=True)
        weights_low = weights.astype(jnp.bfloat16)
        attended = jnp.dot(weights_low, values, preferred_element_type=jnp.float32).astype(
            jnp.bfloat16
        )
        row_delta = jnp.sum(
            do.astype(jnp.float32) * attended.astype(jnp.float32), axis=1, keepdims=True
        )
        weight_grad = lax.dot_general(do, values, nt, preferred_element_type=jnp.float32)
        score_grad = (weights * (weight_grad - row_delta)).astype(jnp.bfloat16)
        query_grad = (
            score_scale * jnp.dot(score_grad, keys, preferred_element_type=jnp.float32)
        ).astype(jnp.bfloat16)
        for a, cols in enumerate(heads):
            o_ref[:, cols] = attended[a * query_rows : (a + 1) * query_rows]
            dq_ref[:, cols] = query_grad[a * query_rows : (a + 1) * query_rows]
        key_piece = (
            score_scale * lax.dot_general(score_grad, q, tn, preferred_element_type=jnp.float32)
        ).astype(jnp.bfloat16)
        value_piece = lax.dot_general(
            weights_low, do, tn, preferred_element_type=jnp.float32
        ).astype(jnp.bfloat16)
        group = pl.program_id(0)
        for index in range(local_groups):

            @pl.when(group == index)
            def _():
                key_cols = slice(index * HEAD_SIZE, (index + 1) * HEAD_SIZE)
                value_cols = slice((local_groups + index) * HEAD_SIZE, (local_groups + index + 1) * HEAD_SIZE)
                pieces_ref[:, key_cols] = key_piece
                pieces_ref[:, value_cols] = value_piece

    return kernel


def attend_all(queries, output_gradient, fetched, count, chunk_rows):
    query_rows, query_width = queries.shape
    key_total, both_width = fetched.shape
    key_width = both_width // 2
    local_groups = key_width // HEAD_SIZE
    heads_per_group = QUERY_HEADS // KEY_VALUE_HEADS
    group_width = heads_per_group * HEAD_SIZE
    row_block = pl.BlockSpec((query_rows, group_width), lambda g: (0, g))
    key_block = pl.BlockSpec((key_total, HEAD_SIZE), lambda g: (0, g))
    value_block = pl.BlockSpec((key_total, HEAD_SIZE), lambda g: (0, local_groups + g))
    return pl.pallas_call(
        attention_kernel(chunk_rows, heads_per_group, local_groups),
        grid=(local_groups,),
        in_specs=[
            pl.BlockSpec(memory_space=pltpu.SMEM),
            row_block,
            row_block,
            key_block,
            value_block,
        ],
        out_specs=[row_block, row_block, pl.BlockSpec((key_total, both_width), lambda g: (0, 0))],
        out_shape=[
            jax.ShapeDtypeStruct((query_rows, query_width), jnp.bfloat16),
            jax.ShapeDtypeStruct((query_rows, query_width), jnp.bfloat16),
            jax.ShapeDtypeStruct((key_total, both_width), jnp.bfloat16),
        ],
    )(count, queries, output_gradient, fetched, fetched)


def make_shards(peers):
    def shards(
        queries, episode_key_cache, episode_value_cache, output_gradient, block_lists, block_counts
    ):
        row_count = episode_key_cache.shape[0]
        key_width = episode_key_cache.shape[2]
        both_width = 2 * key_width
        chunk_rows = row_count // peers

        held = jnp.concatenate(
            [episode_key_cache[:, 0, :], episode_value_cache[:, 0, :]], axis=1
        )
        tag = jnp.concatenate([block_lists[0], block_counts]).astype(jnp.bfloat16)
        tag_block = jnp.broadcast_to(
            jnp.pad(tag, (0, TAG_COLUMNS - LIST - 1)), (row_count, TAG_COLUMNS)
        )
        first_send = jnp.concatenate([held, tag_block], axis=1).reshape(
            peers, chunk_rows, both_width + TAG_COLUMNS
        )
        first_recv = lax.all_to_all(first_send, "ctx", 0, 0, tiled=True)
        info = first_recv[:, 0, both_width : both_width + LIST + 1].astype(jnp.int32)
        lists_all = info[:, :LIST]
        counts_all = info[:, LIST]

        rows_held = first_recv[:, :, :both_width]
        picked = jnp.take(rows_held, lists_all, axis=0, mode="clip").reshape(
            peers, LIST * chunk_rows, both_width
        )
        fetched = lax.all_to_all(picked, "ctx", 0, 0, tiled=True).reshape(
            LIST * row_count, both_width
        )
        attn_out, query_grad, pieces = attend_all(
            queries,
            output_gradient,
            fetched,
            block_counts,
            chunk_rows,
        )

        back = lax.all_to_all(
            pieces.reshape(peers, LIST * chunk_rows, both_width), "ctx", 0, 0, tiled=True
        ).reshape(peers, LIST, chunk_rows, both_width)
        slot_live = jnp.arange(LIST, dtype=jnp.int32)[None, :] < counts_all[:, None]
        selector = (
            (lists_all[:, :, None] == jnp.arange(peers, dtype=jnp.int32)[None, None, :])
            & slot_live[:, :, None]
        ).astype(jnp.bfloat16)
        summed = jnp.einsum(
            "qjrc,qjn->nrc", back, selector, preferred_element_type=jnp.float32
        ).astype(jnp.bfloat16)

        owned = lax.all_to_all(summed, "ctx", 0, 0, tiled=True).reshape(row_count, both_width)
        key_cache_gradient = owned[:, None, :key_width]
        value_cache_gradient = owned[:, None, key_width:]
        return attn_out, query_grad, key_cache_gradient, value_cache_gradient

    return shards


def solution(mesh):
    placed = (
        P(("parts", "ctx"), "tp"),
        P(None, ("parts", "ctx"), "tp"),
        P(None, ("parts", "ctx"), "tp"),
        P(("parts", "ctx"), "tp"),
        P(("parts", "ctx"), None),
        P(("parts", "ctx")),
    )
    return jax.shard_map(
        make_shards(mesh.shape["ctx"]),
        mesh=mesh,
        in_specs=placed,
        out_specs=(
            P(("parts", "ctx"), "tp"),
            P(("parts", "ctx"), "tp"),
            P(None, ("parts", "ctx"), "tp"),
            P(None, ("parts", "ctx"), "tp"),
        ),
        check_vma=False,
    )
```

```python
import jax
import jax.numpy as jnp
from jax import lax
from jax.experimental import pallas as pl
from jax.experimental.pallas import tpu as pltpu
from jax.sharding import PartitionSpec as P

QUERY_HEADS = 64
KEY_VALUE_HEADS = 8
HEAD_SIZE = 128
LIST = 2
TAG_COLUMNS = 128
GROUPS_PER_STEP = 4


def attention_kernel(chunk_rows, heads_per_group, local_groups, groups_per_step):
    score_scale = HEAD_SIZE ** (-0.5)
    group_width = heads_per_group * HEAD_SIZE

    def one_group(live, q_ref, do_ref, k_ref, v_ref, o_ref, dq_ref, within):
        key_cols = slice(within * HEAD_SIZE, (within + 1) * HEAD_SIZE)
        keys = k_ref[:, key_cols]
        values = v_ref[:, key_cols]
        query_rows = q_ref.shape[0]
        nt = (((1,), (1,)), ((), ()))
        tn = (((0,), (0,)), ((), ()))
        heads = [
            slice(within * group_width + a * HEAD_SIZE, within * group_width + (a + 1) * HEAD_SIZE)
            for a in range(heads_per_group)
        ]
        q = jnp.concatenate([q_ref[:, cols] for cols in heads], axis=0)
        do = jnp.concatenate([do_ref[:, cols] for cols in heads], axis=0)
        scores = score_scale * lax.dot_general(q, keys, nt, preferred_element_type=jnp.float32)
        masked = jnp.where(live, scores, -jnp.inf)
        peak = jnp.max(masked, axis=1, keepdims=True)
        exponent = jnp.exp(masked - peak)
        weights = exponent / jnp.sum(exponent, axis=1, keepdims=True)
        weights_low = weights.astype(jnp.bfloat16)
        attended = jnp.dot(weights_low, values, preferred_element_type=jnp.float32).astype(
            jnp.bfloat16
        )
        row_delta = jnp.sum(
            do.astype(jnp.float32) * attended.astype(jnp.float32), axis=1, keepdims=True
        )
        weight_grad = lax.dot_general(do, values, nt, preferred_element_type=jnp.float32)
        score_grad = (weights * (weight_grad - row_delta)).astype(jnp.bfloat16)
        query_grad = (
            score_scale * jnp.dot(score_grad, keys, preferred_element_type=jnp.float32)
        ).astype(jnp.bfloat16)
        for a, cols in enumerate(heads):
            o_ref[:, cols] = attended[a * query_rows : (a + 1) * query_rows]
            dq_ref[:, cols] = query_grad[a * query_rows : (a + 1) * query_rows]
        key_piece = (
            score_scale * lax.dot_general(score_grad, q, tn, preferred_element_type=jnp.float32)
        ).astype(jnp.bfloat16)
        value_piece = lax.dot_general(
            weights_low, do, tn, preferred_element_type=jnp.float32
        ).astype(jnp.bfloat16)
        return key_piece, value_piece

    def kernel(count_ref, q_ref, do_ref, k_ref, v_ref, o_ref, dq_ref, pieces_ref):
        key_total = k_ref.shape[0]
        slot = (lax.broadcasted_iota(jnp.int32, (1, key_total), 1) // chunk_rows) % LIST
        live = slot < count_ref[0]
        pieces = [
            one_group(live, q_ref, do_ref, k_ref, v_ref, o_ref, dq_ref, within)
            for within in range(groups_per_step)
        ]
        step = pl.program_id(0)
        for index in range(local_groups // groups_per_step):

            @pl.when(step == index)
            def _():
                for within, (key_piece, value_piece) in enumerate(pieces):
                    group = index * groups_per_step + within
                    key_cols = slice(group * HEAD_SIZE, (group + 1) * HEAD_SIZE)
                    value_cols = slice(
                        (local_groups + group) * HEAD_SIZE, (local_groups + group + 1) * HEAD_SIZE
                    )
                    pieces_ref[:, key_cols] = key_piece
                    pieces_ref[:, value_cols] = value_piece

    return kernel


def attend_all(queries, output_gradient, fetched, count, chunk_rows, groups_per_step=GROUPS_PER_STEP):
    query_rows, query_width = queries.shape
    key_total, both_width = fetched.shape
    key_width = both_width // 2
    local_groups = key_width // HEAD_SIZE
    groups_per_step = min(groups_per_step, local_groups)
    steps = local_groups // groups_per_step
    heads_per_group = QUERY_HEADS // KEY_VALUE_HEADS
    step_width = groups_per_step * heads_per_group * HEAD_SIZE
    key_step = groups_per_step * HEAD_SIZE
    row_block = pl.BlockSpec((query_rows, step_width), lambda i: (0, i))
    key_block = pl.BlockSpec((key_total, key_step), lambda i: (0, i))
    value_block = pl.BlockSpec((key_total, key_step), lambda i: (0, steps + i))
    return pl.pallas_call(
        attention_kernel(chunk_rows, heads_per_group, local_groups, groups_per_step),
        grid=(steps,),
        in_specs=[
            pl.BlockSpec(memory_space=pltpu.SMEM),
            row_block,
            row_block,
            key_block,
            value_block,
        ],
        out_specs=[row_block, row_block, pl.BlockSpec((key_total, both_width), lambda i: (0, 0))],
        out_shape=[
            jax.ShapeDtypeStruct((query_rows, query_width), jnp.bfloat16),
            jax.ShapeDtypeStruct((query_rows, query_width), jnp.bfloat16),
            jax.ShapeDtypeStruct((key_total, both_width), jnp.bfloat16),
        ],
    )(count, queries, output_gradient, fetched, fetched)


def make_shards(peers):
    def shards(
        queries, episode_key_cache, episode_value_cache, output_gradient, block_lists, block_counts
    ):
        row_count = episode_key_cache.shape[0]
        key_width = episode_key_cache.shape[2]
        both_width = 2 * key_width
        chunk_rows = row_count // peers

        held = jnp.concatenate(
            [episode_key_cache[:, 0, :], episode_value_cache[:, 0, :]], axis=1
        )
        tag = jnp.concatenate([block_lists[0], block_counts]).astype(jnp.bfloat16)
        tag_block = jnp.broadcast_to(
            jnp.pad(tag, (0, TAG_COLUMNS - LIST - 1)), (row_count, TAG_COLUMNS)
        )
        first_send = jnp.concatenate([held, tag_block], axis=1).reshape(
            peers, chunk_rows, both_width + TAG_COLUMNS
        )
        first_recv = lax.all_to_all(first_send, "ctx", 0, 0, tiled=True)
        info = first_recv[:, 0, both_width : both_width + LIST + 1].astype(jnp.int32)
        lists_all = info[:, :LIST]
        counts_all = info[:, LIST]

        rows_held = first_recv[:, :, :both_width]
        picked = jnp.take(rows_held, lists_all, axis=0, mode="clip").reshape(
            peers, LIST * chunk_rows, both_width
        )
        fetched = lax.all_to_all(picked, "ctx", 0, 0, tiled=True).reshape(
            LIST * row_count, both_width
        )
        attn_out, query_grad, pieces = attend_all(
            queries,
            output_gradient,
            fetched,
            block_counts,
            chunk_rows,
        )

        back = lax.all_to_all(
            pieces.reshape(peers, LIST * chunk_rows, both_width), "ctx", 0, 0, tiled=True
        ).reshape(peers, LIST, chunk_rows, both_width)
        slot_live = jnp.arange(LIST, dtype=jnp.int32)[None, :] < counts_all[:, None]
        selector = (
            (lists_all[:, :, None] == jnp.arange(peers, dtype=jnp.int32)[None, None, :])
            & slot_live[:, :, None]
        ).astype(jnp.bfloat16)
        summed = jnp.einsum(
            "qjrc,qjn->nrc", back, selector, preferred_element_type=jnp.float32
        ).astype(jnp.bfloat16)

        owned = lax.all_to_all(summed, "ctx", 0, 0, tiled=True).reshape(row_count, both_width)
        key_cache_gradient = owned[:, None, :key_width]
        value_cache_gradient = owned[:, None, key_width:]
        return attn_out, query_grad, key_cache_gradient, value_cache_gradient

    return shards


def solution(mesh):
    placed = (
        P(("parts", "ctx"), "tp"),
        P(None, ("parts", "ctx"), "tp"),
        P(None, ("parts", "ctx"), "tp"),
        P(("parts", "ctx"), "tp"),
        P(("parts", "ctx"), None),
        P(("parts", "ctx")),
    )
    return jax.shard_map(
        make_shards(mesh.shape["ctx"]),
        mesh=mesh,
        in_specs=placed,
        out_specs=(
            P(("parts", "ctx"), "tp"),
            P(("parts", "ctx"), "tp"),
            P(None, ("parts", "ctx"), "tp"),
            P(None, ("parts", "ctx"), "tp"),
        ),
        check_vma=False,
    )
```

```python
import jax
import jax.numpy as jnp
from jax import lax
from jax.experimental import pallas as pl
from jax.experimental.pallas import tpu as pltpu
from jax.sharding import PartitionSpec as P

QUERY_HEADS = 64
KEY_VALUE_HEADS = 8
HEAD_SIZE = 128
LIST = 2
TAG_COLUMNS = 128
GROUPS_PER_STEP = 4


def attention_kernel(chunk_rows, heads_per_group, local_groups, groups_per_step):
    score_scale = HEAD_SIZE ** (-0.5)
    group_width = heads_per_group * HEAD_SIZE

    def one_group(live, q_ref, do_ref, k_ref, v_ref, o_ref, dq_ref, within):
        key_cols = slice(within * HEAD_SIZE, (within + 1) * HEAD_SIZE)
        keys = k_ref[:, key_cols]
        values = v_ref[:, key_cols]
        query_rows = q_ref.shape[0]
        nt = (((1,), (1,)), ((), ()))
        tn = (((0,), (0,)), ((), ()))
        heads = [
            slice(within * group_width + a * HEAD_SIZE, within * group_width + (a + 1) * HEAD_SIZE)
            for a in range(heads_per_group)
        ]
        q = jnp.concatenate([q_ref[:, cols] for cols in heads], axis=0)
        do = jnp.concatenate([do_ref[:, cols] for cols in heads], axis=0)
        scores = score_scale * lax.dot_general(q, keys, nt, preferred_element_type=jnp.float32)
        masked = jnp.where(live, scores, -jnp.inf)
        peak = jnp.max(masked, axis=1, keepdims=True)
        exponent = jnp.exp(masked - peak)
        weights = exponent / jnp.sum(exponent, axis=1, keepdims=True)
        weights_low = weights.astype(jnp.bfloat16)
        attended = jnp.dot(weights_low, values, preferred_element_type=jnp.float32).astype(
            jnp.bfloat16
        )
        row_delta = jnp.sum(
            do.astype(jnp.float32) * attended.astype(jnp.float32), axis=1, keepdims=True
        )
        weight_grad = lax.dot_general(do, values, nt, preferred_element_type=jnp.float32)
        score_grad = (weights * (weight_grad - row_delta)).astype(jnp.bfloat16)
        query_grad = (
            score_scale * jnp.dot(score_grad, keys, preferred_element_type=jnp.float32)
        ).astype(jnp.bfloat16)
        for a, cols in enumerate(heads):
            o_ref[:, cols] = attended[a * query_rows : (a + 1) * query_rows]
            dq_ref[:, cols] = query_grad[a * query_rows : (a + 1) * query_rows]
        key_piece = (
            score_scale * lax.dot_general(score_grad, q, tn, preferred_element_type=jnp.float32)
        ).astype(jnp.bfloat16)
        value_piece = lax.dot_general(
            weights_low, do, tn, preferred_element_type=jnp.float32
        ).astype(jnp.bfloat16)
        return key_piece, value_piece

    def kernel(count_ref, q_ref, do_ref, k_ref, v_ref, o_ref, dq_ref, pieces_ref):
        key_total = k_ref.shape[0]
        slot = (lax.broadcasted_iota(jnp.int32, (1, key_total), 1) // chunk_rows) % LIST
        live = slot < count_ref[0]
        pieces = [
            one_group(live, q_ref, do_ref, k_ref, v_ref, o_ref, dq_ref, within)
            for within in range(groups_per_step)
        ]
        step = pl.program_id(0)
        for index in range(local_groups // groups_per_step):

            @pl.when(step == index)
            def _():
                for within, (key_piece, value_piece) in enumerate(pieces):
                    group = index * groups_per_step + within
                    key_cols = slice(group * HEAD_SIZE, (group + 1) * HEAD_SIZE)
                    value_cols = slice(
                        (local_groups + group) * HEAD_SIZE, (local_groups + group + 1) * HEAD_SIZE
                    )
                    pieces_ref[:, key_cols] = key_piece
                    pieces_ref[:, value_cols] = value_piece

    return kernel


def attend_all(queries, output_gradient, fetched, count, chunk_rows, groups_per_step=GROUPS_PER_STEP):
    query_rows, query_width = queries.shape
    key_total, both_width = fetched.shape
    key_width = both_width // 2
    local_groups = key_width // HEAD_SIZE
    groups_per_step = min(groups_per_step, local_groups)
    steps = local_groups // groups_per_step
    heads_per_group = QUERY_HEADS // KEY_VALUE_HEADS
    step_width = groups_per_step * heads_per_group * HEAD_SIZE
    key_step = groups_per_step * HEAD_SIZE
    row_block = pl.BlockSpec((query_rows, step_width), lambda i: (0, i))
    key_block = pl.BlockSpec((key_total, key_step), lambda i: (0, i))
    value_block = pl.BlockSpec((key_total, key_step), lambda i: (0, steps + i))
    return pl.pallas_call(
        attention_kernel(chunk_rows, heads_per_group, local_groups, groups_per_step),
        grid=(steps,),
        in_specs=[
            pl.BlockSpec(memory_space=pltpu.SMEM),
            row_block,
            row_block,
            key_block,
            value_block,
        ],
        out_specs=[row_block, row_block, pl.BlockSpec((key_total, both_width), lambda i: (0, 0))],
        out_shape=[
            jax.ShapeDtypeStruct((query_rows, query_width), jnp.bfloat16),
            jax.ShapeDtypeStruct((query_rows, query_width), jnp.bfloat16),
            jax.ShapeDtypeStruct((key_total, both_width), jnp.bfloat16),
        ],
    )(count, queries, output_gradient, fetched, fetched)


def pack_kernel(list_ref, count_ref, k_ref, v_ref, out_ref):
    key_width = k_ref.shape[1]
    out_ref[:, :key_width] = k_ref[...]
    out_ref[:, key_width : 2 * key_width] = v_ref[...]
    lane = lax.broadcasted_iota(jnp.int32, (k_ref.shape[0], TAG_COLUMNS), 1)
    tag = jnp.where(lane == 0, list_ref[0, 0], 0)
    tag = jnp.where(lane == 1, list_ref[0, 1], tag)
    tag = jnp.where(lane == LIST, count_ref[0], tag)
    out_ref[:, 2 * key_width :] = tag.astype(jnp.float32).astype(jnp.bfloat16)


def pack_rows(keys, values, block_lists, block_counts):
    row_count, key_width = keys.shape
    whole = lambda shape: pl.BlockSpec(shape, lambda: (0, 0))
    return pl.pallas_call(
        pack_kernel,
        in_specs=[
            pl.BlockSpec(memory_space=pltpu.SMEM),
            pl.BlockSpec(memory_space=pltpu.SMEM),
            whole((row_count, key_width)),
            whole((row_count, key_width)),
        ],
        out_specs=whole((row_count, 2 * key_width + TAG_COLUMNS)),
        out_shape=jax.ShapeDtypeStruct((row_count, 2 * key_width + TAG_COLUMNS), jnp.bfloat16),
    )(block_lists, block_counts, keys, values)


def make_shards(peers):
    def shards(
        queries, episode_key_cache, episode_value_cache, output_gradient, block_lists, block_counts
    ):
        row_count = episode_key_cache.shape[0]
        key_width = episode_key_cache.shape[2]
        both_width = 2 * key_width
        chunk_rows = row_count // peers

        first_send = pack_rows(
            episode_key_cache.reshape(row_count, key_width),
            episode_value_cache.reshape(row_count, key_width),
            block_lists,
            block_counts,
        ).reshape(peers, chunk_rows, both_width + TAG_COLUMNS)
        first_recv = lax.all_to_all(first_send, "ctx", 0, 0, tiled=True)
        info = first_recv[:, 0, both_width : both_width + LIST + 1].astype(jnp.int32)
        lists_all = info[:, :LIST]
        counts_all = info[:, LIST]

        rows_held = first_recv[:, :, :both_width]
        picked = jnp.take(rows_held, lists_all, axis=0, mode="clip").reshape(
            peers, LIST * chunk_rows, both_width
        )
        fetched = lax.all_to_all(picked, "ctx", 0, 0, tiled=True).reshape(
            LIST * row_count, both_width
        )
        attn_out, query_grad, pieces = attend_all(
            queries,
            output_gradient,
            fetched,
            block_counts,
            chunk_rows,
        )

        back = lax.all_to_all(
            pieces.reshape(peers, LIST * chunk_rows, both_width), "ctx", 0, 0, tiled=True
        ).reshape(peers, LIST, chunk_rows, both_width)
        slot_live = jnp.arange(LIST, dtype=jnp.int32)[None, :] < counts_all[:, None]
        selector = (
            (lists_all[:, :, None] == jnp.arange(peers, dtype=jnp.int32)[None, None, :])
            & slot_live[:, :, None]
        ).astype(jnp.bfloat16)
        summed = jnp.einsum(
            "qjrc,qjn->nrc", back, selector, preferred_element_type=jnp.float32
        ).astype(jnp.bfloat16)

        owned = lax.all_to_all(summed, "ctx", 0, 0, tiled=True).reshape(row_count, both_width)
        key_cache_gradient = owned[:, None, :key_width]
        value_cache_gradient = owned[:, None, key_width:]
        return attn_out, query_grad, key_cache_gradient, value_cache_gradient

    return shards


def solution(mesh):
    placed = (
        P(("parts", "ctx"), "tp"),
        P(None, ("parts", "ctx"), "tp"),
        P(None, ("parts", "ctx"), "tp"),
        P(("parts", "ctx"), "tp"),
        P(("parts", "ctx"), None),
        P(("parts", "ctx")),
    )
    return jax.shard_map(
        make_shards(mesh.shape["ctx"]),
        mesh=mesh,
        in_specs=placed,
        out_specs=(
            P(("parts", "ctx"), "tp"),
            P(("parts", "ctx"), "tp"),
            P(None, ("parts", "ctx"), "tp"),
            P(None, ("parts", "ctx"), "tp"),
        ),
        check_vma=False,
    )
```

```python
import jax
import jax.numpy as jnp
from jax import lax
from jax.experimental import pallas as pl
from jax.experimental.pallas import tpu as pltpu
from jax.sharding import PartitionSpec as P

QUERY_HEADS = 64
KEY_VALUE_HEADS = 8
HEAD_SIZE = 128
LIST = 2
TAG_COLUMNS = 128
GROUPS_PER_STEP = 4


def attention_kernel(chunk_rows, heads_per_group, local_groups, groups_per_step, pieces_only):
    score_scale = HEAD_SIZE ** (-0.5)
    group_width = heads_per_group * HEAD_SIZE

    def one_group(live, q_ref, do_ref, k_ref, v_ref, o_ref, dq_ref, within):
        key_cols = slice(within * HEAD_SIZE, (within + 1) * HEAD_SIZE)
        keys = k_ref[:, key_cols]
        values = v_ref[:, key_cols]
        query_rows = q_ref.shape[0]
        nt = (((1,), (1,)), ((), ()))
        tn = (((0,), (0,)), ((), ()))
        heads = [
            slice(within * group_width + a * HEAD_SIZE, within * group_width + (a + 1) * HEAD_SIZE)
            for a in range(heads_per_group)
        ]
        q = jnp.concatenate([q_ref[:, cols] for cols in heads], axis=0)
        do = jnp.concatenate([do_ref[:, cols] for cols in heads], axis=0)
        scores = score_scale * lax.dot_general(q, keys, nt, preferred_element_type=jnp.float32)
        masked = jnp.where(live, scores, -jnp.inf)
        peak = jnp.max(masked, axis=1, keepdims=True)
        exponent = jnp.exp(masked - peak)
        weights = exponent / jnp.sum(exponent, axis=1, keepdims=True)
        weights_low = weights.astype(jnp.bfloat16)
        attended = jnp.dot(weights_low, values, preferred_element_type=jnp.float32).astype(
            jnp.bfloat16
        )
        row_delta = jnp.sum(
            do.astype(jnp.float32) * attended.astype(jnp.float32), axis=1, keepdims=True
        )
        weight_grad = lax.dot_general(do, values, nt, preferred_element_type=jnp.float32)
        score_grad = (weights * (weight_grad - row_delta)).astype(jnp.bfloat16)
        if not pieces_only:
            query_grad = (
                score_scale * jnp.dot(score_grad, keys, preferred_element_type=jnp.float32)
            ).astype(jnp.bfloat16)
            for a, cols in enumerate(heads):
                o_ref[:, cols] = attended[a * query_rows : (a + 1) * query_rows]
                dq_ref[:, cols] = query_grad[a * query_rows : (a + 1) * query_rows]
            return None
        key_piece = (
            score_scale * lax.dot_general(score_grad, q, tn, preferred_element_type=jnp.float32)
        ).astype(jnp.bfloat16)
        value_piece = lax.dot_general(
            weights_low, do, tn, preferred_element_type=jnp.float32
        ).astype(jnp.bfloat16)
        return key_piece, value_piece

    def kernel(count_ref, q_ref, do_ref, k_ref, v_ref, *out_refs):
        key_total = k_ref.shape[0]
        slot = (lax.broadcasted_iota(jnp.int32, (1, key_total), 1) // chunk_rows) % LIST
        live = slot < count_ref[0]
        o_ref, dq_ref = (None, None) if pieces_only else out_refs
        pieces = [
            one_group(live, q_ref, do_ref, k_ref, v_ref, o_ref, dq_ref, within)
            for within in range(groups_per_step)
        ]
        if not pieces_only:
            return
        (pieces_ref,) = out_refs
        step = pl.program_id(0)
        for index in range(local_groups // groups_per_step):

            @pl.when(step == index)
            def _():
                for within, (key_piece, value_piece) in enumerate(pieces):
                    group = index * groups_per_step + within
                    key_cols = slice(group * HEAD_SIZE, (group + 1) * HEAD_SIZE)
                    value_cols = slice(
                        (local_groups + group) * HEAD_SIZE, (local_groups + group + 1) * HEAD_SIZE
                    )
                    pieces_ref[:, key_cols] = key_piece
                    pieces_ref[:, value_cols] = value_piece

    return kernel


def attend_all(queries, output_gradient, fetched, count, chunk_rows, groups_per_step=GROUPS_PER_STEP):
    query_rows, query_width = queries.shape
    key_total, both_width = fetched.shape
    key_width = both_width // 2
    local_groups = key_width // HEAD_SIZE
    groups_per_step = min(groups_per_step, local_groups)
    steps = local_groups // groups_per_step
    heads_per_group = QUERY_HEADS // KEY_VALUE_HEADS
    step_width = groups_per_step * heads_per_group * HEAD_SIZE
    key_step = groups_per_step * HEAD_SIZE
    row_block = pl.BlockSpec((query_rows, step_width), lambda i: (0, i))
    key_block = pl.BlockSpec((key_total, key_step), lambda i: (0, i))
    value_block = pl.BlockSpec((key_total, key_step), lambda i: (0, steps + i))
    in_specs = [pl.BlockSpec(memory_space=pltpu.SMEM), row_block, row_block, key_block, value_block]
    pieces = pl.pallas_call(
        attention_kernel(chunk_rows, heads_per_group, local_groups, groups_per_step, True),
        grid=(steps,),
        in_specs=in_specs,
        out_specs=pl.BlockSpec((key_total, both_width), lambda i: (0, 0)),
        out_shape=jax.ShapeDtypeStruct((key_total, both_width), jnp.bfloat16),
    )(count, queries, output_gradient, fetched, fetched)
    attended, query_grad = pl.pallas_call(
        attention_kernel(chunk_rows, heads_per_group, local_groups, groups_per_step, False),
        grid=(steps,),
        in_specs=in_specs,
        out_specs=[row_block, row_block],
        out_shape=[
            jax.ShapeDtypeStruct((query_rows, query_width), jnp.bfloat16),
            jax.ShapeDtypeStruct((query_rows, query_width), jnp.bfloat16),
        ],
    )(count, queries, output_gradient, fetched, fetched)
    return attended, query_grad, pieces


def make_shards(peers):
    def shards(
        queries, episode_key_cache, episode_value_cache, output_gradient, block_lists, block_counts
    ):
        row_count = episode_key_cache.shape[0]
        key_width = episode_key_cache.shape[2]
        both_width = 2 * key_width
        chunk_rows = row_count // peers

        held = jnp.concatenate(
            [episode_key_cache[:, 0, :], episode_value_cache[:, 0, :]], axis=1
        )
        tag = jnp.concatenate([block_lists[0], block_counts]).astype(jnp.bfloat16)
        tag_block = jnp.broadcast_to(
            jnp.pad(tag, (0, TAG_COLUMNS - LIST - 1)), (row_count, TAG_COLUMNS)
        )
        first_send = jnp.concatenate([held, tag_block], axis=1).reshape(
            peers, chunk_rows, both_width + TAG_COLUMNS
        )
        first_recv = lax.all_to_all(first_send, "ctx", 0, 0, tiled=True)
        info = first_recv[:, 0, both_width : both_width + LIST + 1].astype(jnp.int32)
        lists_all = info[:, :LIST]
        counts_all = info[:, LIST]

        rows_held = first_recv[:, :, :both_width]
        picked = jnp.take(rows_held, lists_all, axis=0, mode="clip").reshape(
            peers, LIST * chunk_rows, both_width
        )
        fetched = lax.all_to_all(picked, "ctx", 0, 0, tiled=True).reshape(
            LIST * row_count, both_width
        )
        attn_out, query_grad, pieces = attend_all(
            queries,
            output_gradient,
            fetched,
            block_counts,
            chunk_rows,
        )

        back = lax.all_to_all(
            pieces.reshape(peers, LIST * chunk_rows, both_width), "ctx", 0, 0, tiled=True
        ).reshape(peers, LIST, chunk_rows, both_width)
        slot_live = jnp.arange(LIST, dtype=jnp.int32)[None, :] < counts_all[:, None]
        selector = (
            (lists_all[:, :, None] == jnp.arange(peers, dtype=jnp.int32)[None, None, :])
            & slot_live[:, :, None]
        ).astype(jnp.bfloat16)
        summed = jnp.einsum(
            "qjrc,qjn->nrc", back, selector, preferred_element_type=jnp.float32
        ).astype(jnp.bfloat16)

        owned = lax.all_to_all(summed, "ctx", 0, 0, tiled=True).reshape(row_count, both_width)
        key_cache_gradient = owned[:, None, :key_width]
        value_cache_gradient = owned[:, None, key_width:]
        return attn_out, query_grad, key_cache_gradient, value_cache_gradient

    return shards


def solution(mesh):
    placed = (
        P(("parts", "ctx"), "tp"),
        P(None, ("parts", "ctx"), "tp"),
        P(None, ("parts", "ctx"), "tp"),
        P(("parts", "ctx"), "tp"),
        P(("parts", "ctx"), None),
        P(("parts", "ctx")),
    )
    return jax.shard_map(
        make_shards(mesh.shape["ctx"]),
        mesh=mesh,
        in_specs=placed,
        out_specs=(
            P(("parts", "ctx"), "tp"),
            P(("parts", "ctx"), "tp"),
            P(None, ("parts", "ctx"), "tp"),
            P(None, ("parts", "ctx"), "tp"),
        ),
        check_vma=False,
    )
```

```python
import jax
import jax.numpy as jnp
from jax import lax
from jax.experimental import pallas as pl
from jax.experimental.pallas import tpu as pltpu
from jax.sharding import PartitionSpec as P

QUERY_HEADS = 64
KEY_VALUE_HEADS = 8
HEAD_SIZE = 128
LIST = 2
TAG_COLUMNS = 128
GROUPS_PER_STEP = 4


def attention_kernel(chunk_rows, heads_per_group, local_groups, groups_per_step):
    score_scale = HEAD_SIZE ** (-0.5)
    group_width = heads_per_group * HEAD_SIZE

    def one_group(live, q_ref, do_ref, k_ref, v_ref, o_ref, dq_ref, within):
        key_cols = slice(within * HEAD_SIZE, (within + 1) * HEAD_SIZE)
        keys = k_ref[:, key_cols]
        values = v_ref[:, key_cols]
        query_rows = q_ref.shape[0]
        nt = (((1,), (1,)), ((), ()))
        tn = (((0,), (0,)), ((), ()))
        heads = [
            slice(within * group_width + a * HEAD_SIZE, within * group_width + (a + 1) * HEAD_SIZE)
            for a in range(heads_per_group)
        ]
        q = jnp.concatenate([q_ref[:, cols] for cols in heads], axis=0)
        do = jnp.concatenate([do_ref[:, cols] for cols in heads], axis=0)
        scores = score_scale * lax.dot_general(q, keys, nt, preferred_element_type=jnp.float32)
        masked = jnp.where(live, scores, -jnp.inf)
        peak = jnp.max(masked, axis=1, keepdims=True)
        exponent = jnp.exp(masked - peak)
        weights = exponent / jnp.sum(exponent, axis=1, keepdims=True)
        weights_low = weights.astype(jnp.bfloat16)
        attended = jnp.dot(weights_low, values, preferred_element_type=jnp.float32).astype(
            jnp.bfloat16
        )
        row_delta = jnp.sum(
            do.astype(jnp.float32) * attended.astype(jnp.float32), axis=1, keepdims=True
        )
        weight_grad = lax.dot_general(do, values, nt, preferred_element_type=jnp.float32)
        score_grad = (weights * (weight_grad - row_delta)).astype(jnp.bfloat16)
        query_grad = (
            score_scale * jnp.dot(score_grad, keys, preferred_element_type=jnp.float32)
        ).astype(jnp.bfloat16)
        for a, cols in enumerate(heads):
            o_ref[:, cols] = attended[a * query_rows : (a + 1) * query_rows]
            dq_ref[:, cols] = query_grad[a * query_rows : (a + 1) * query_rows]
        key_piece = (
            score_scale * lax.dot_general(score_grad, q, tn, preferred_element_type=jnp.float32)
        ).astype(jnp.bfloat16)
        value_piece = lax.dot_general(
            weights_low, do, tn, preferred_element_type=jnp.float32
        ).astype(jnp.bfloat16)
        return key_piece, value_piece

    def kernel(count_ref, q_ref, do_ref, k_ref, v_ref, o_ref, dq_ref, pieces_ref):
        key_total = k_ref.shape[0]
        slot = (lax.broadcasted_iota(jnp.int32, (1, key_total), 1) // chunk_rows) % LIST
        live = slot < count_ref[0]
        pieces = [
            one_group(live, q_ref, do_ref, k_ref, v_ref, o_ref, dq_ref, within)
            for within in range(groups_per_step)
        ]
        step = pl.program_id(0)
        for index in range(local_groups // groups_per_step):

            @pl.when(step == index)
            def _():
                for within, (key_piece, value_piece) in enumerate(pieces):
                    group = index * groups_per_step + within
                    key_cols = slice(group * HEAD_SIZE, (group + 1) * HEAD_SIZE)
                    value_cols = slice(
                        (local_groups + group) * HEAD_SIZE, (local_groups + group + 1) * HEAD_SIZE
                    )
                    pieces_ref[:, key_cols] = key_piece
                    pieces_ref[:, value_cols] = value_piece

    return kernel


def attend_all(queries, output_gradient, fetched, count, chunk_rows, groups_per_step=GROUPS_PER_STEP):
    query_rows, query_width = queries.shape
    key_total, both_width = fetched.shape
    key_width = both_width // 2
    local_groups = key_width // HEAD_SIZE
    groups_per_step = min(groups_per_step, local_groups)
    steps = local_groups // groups_per_step
    heads_per_group = QUERY_HEADS // KEY_VALUE_HEADS
    step_width = groups_per_step * heads_per_group * HEAD_SIZE
    key_step = groups_per_step * HEAD_SIZE
    row_block = pl.BlockSpec((query_rows, step_width), lambda i: (0, i))
    key_block = pl.BlockSpec((key_total, key_step), lambda i: (0, i))
    value_block = pl.BlockSpec((key_total, key_step), lambda i: (0, steps + i))
    return pl.pallas_call(
        attention_kernel(chunk_rows, heads_per_group, local_groups, groups_per_step),
        grid=(steps,),
        in_specs=[
            pl.BlockSpec(memory_space=pltpu.SMEM),
            row_block,
            row_block,
            key_block,
            value_block,
        ],
        out_specs=[row_block, row_block, pl.BlockSpec((key_total, both_width), lambda i: (0, 0))],
        out_shape=[
            jax.ShapeDtypeStruct((query_rows, query_width), jnp.bfloat16),
            jax.ShapeDtypeStruct((query_rows, query_width), jnp.bfloat16),
            jax.ShapeDtypeStruct((key_total, both_width), jnp.bfloat16),
        ],
    )(count, queries, output_gradient, fetched, fetched)


def make_shards(peers):
    def shards(
        queries, episode_key_cache, episode_value_cache, output_gradient, block_lists, block_counts
    ):
        row_count = episode_key_cache.shape[0]
        key_width = episode_key_cache.shape[2]
        both_width = 2 * key_width
        chunk_rows = row_count // peers

        held = jnp.concatenate(
            [episode_key_cache[:, 0, :], episode_value_cache[:, 0, :]], axis=1
        )
        first_send, listed, counted = lax.optimization_barrier(
            (jnp.pad(held, ((0, 0), (0, TAG_COLUMNS))), block_lists, block_counts)
        )
        tag = jnp.concatenate([listed[0], counted]).astype(jnp.bfloat16)
        tag_block = jnp.broadcast_to(
            jnp.pad(tag, (0, TAG_COLUMNS - LIST - 1)), (row_count, TAG_COLUMNS)
        )
        first_send = lax.dynamic_update_slice(first_send, tag_block, (0, both_width)).reshape(
            peers, chunk_rows, both_width + TAG_COLUMNS
        )
        first_recv = lax.all_to_all(first_send, "ctx", 0, 0, tiled=True)
        info = first_recv[:, 0, both_width : both_width + LIST + 1].astype(jnp.int32)
        lists_all = info[:, :LIST]
        counts_all = info[:, LIST]

        rows_held = first_recv[:, :, :both_width]
        picked = jnp.take(rows_held, lists_all, axis=0, mode="clip").reshape(
            peers, LIST * chunk_rows, both_width
        )
        fetched = lax.all_to_all(picked, "ctx", 0, 0, tiled=True).reshape(
            LIST * row_count, both_width
        )
        attn_out, query_grad, pieces = attend_all(
            queries,
            output_gradient,
            fetched,
            block_counts,
            chunk_rows,
        )

        back = lax.all_to_all(
            pieces.reshape(peers, LIST * chunk_rows, both_width), "ctx", 0, 0, tiled=True
        ).reshape(peers, LIST, chunk_rows, both_width)
        slot_live = jnp.arange(LIST, dtype=jnp.int32)[None, :] < counts_all[:, None]
        selector = (
            (lists_all[:, :, None] == jnp.arange(peers, dtype=jnp.int32)[None, None, :])
            & slot_live[:, :, None]
        ).astype(jnp.bfloat16)
        summed = jnp.einsum(
            "qjrc,qjn->nrc", back, selector, preferred_element_type=jnp.float32
        ).astype(jnp.bfloat16)

        owned = lax.all_to_all(summed, "ctx", 0, 0, tiled=True).reshape(row_count, both_width)
        key_cache_gradient = owned[:, None, :key_width]
        value_cache_gradient = owned[:, None, key_width:]
        return attn_out, query_grad, key_cache_gradient, value_cache_gradient

    return shards


def solution(mesh):
    placed = (
        P(("parts", "ctx"), "tp"),
        P(None, ("parts", "ctx"), "tp"),
        P(None, ("parts", "ctx"), "tp"),
        P(("parts", "ctx"), "tp"),
        P(("parts", "ctx"), None),
        P(("parts", "ctx")),
    )
    return jax.shard_map(
        make_shards(mesh.shape["ctx"]),
        mesh=mesh,
        in_specs=placed,
        out_specs=(
            P(("parts", "ctx"), "tp"),
            P(("parts", "ctx"), "tp"),
            P(None, ("parts", "ctx"), "tp"),
            P(None, ("parts", "ctx"), "tp"),
        ),
        check_vma=False,
    )
```

```python
import jax
import jax.numpy as jnp
from jax import lax
from jax.experimental import pallas as pl
from jax.experimental.pallas import tpu as pltpu
from jax.sharding import PartitionSpec as P

QUERY_HEADS = 64
KEY_VALUE_HEADS = 8
HEAD_SIZE = 128
LIST = 2
TAG_COLUMNS = 128
GROUPS_PER_STEP = 4


def attention_kernel(chunk_rows, heads_per_group, local_groups, groups_per_step):
    score_scale = HEAD_SIZE ** (-0.5)
    group_width = heads_per_group * HEAD_SIZE

    def one_group(live, q_ref, do_ref, k_ref, v_ref, o_ref, dq_ref, within):
        key_cols = slice(within * HEAD_SIZE, (within + 1) * HEAD_SIZE)
        keys = k_ref[:, key_cols]
        values = v_ref[:, key_cols]
        query_rows = q_ref.shape[0]
        nt = (((1,), (1,)), ((), ()))
        tn = (((0,), (0,)), ((), ()))
        heads = [
            slice(within * group_width + a * HEAD_SIZE, within * group_width + (a + 1) * HEAD_SIZE)
            for a in range(heads_per_group)
        ]
        q = jnp.concatenate([q_ref[:, cols] for cols in heads], axis=0)
        do = jnp.concatenate([do_ref[:, cols] for cols in heads], axis=0)
        scores = score_scale * lax.dot_general(q, keys, nt, preferred_element_type=jnp.float32)
        masked = jnp.where(live, scores, -jnp.inf)
        peak = jnp.max(masked, axis=1, keepdims=True)
        exponent = jnp.exp(masked - peak)
        weights = exponent / jnp.sum(exponent, axis=1, keepdims=True)
        weights_low = weights.astype(jnp.bfloat16)
        attended = jnp.dot(weights_low, values, preferred_element_type=jnp.float32).astype(
            jnp.bfloat16
        )
        row_delta = jnp.sum(
            do.astype(jnp.float32) * attended.astype(jnp.float32), axis=1, keepdims=True
        )
        weight_grad = lax.dot_general(do, values, nt, preferred_element_type=jnp.float32)
        score_grad = (weights * (weight_grad - row_delta)).astype(jnp.bfloat16)
        query_grad = (
            score_scale * jnp.dot(score_grad, keys, preferred_element_type=jnp.float32)
        ).astype(jnp.bfloat16)
        for a, cols in enumerate(heads):
            o_ref[:, cols] = attended[a * query_rows : (a + 1) * query_rows]
            dq_ref[:, cols] = query_grad[a * query_rows : (a + 1) * query_rows]
        key_piece = (
            score_scale * lax.dot_general(score_grad, q, tn, preferred_element_type=jnp.float32)
        ).astype(jnp.bfloat16)
        value_piece = lax.dot_general(
            weights_low, do, tn, preferred_element_type=jnp.float32
        ).astype(jnp.bfloat16)
        return key_piece, value_piece

    def kernel(count_ref, q_ref, do_ref, k_ref, v_ref, o_ref, dq_ref, pieces_ref):
        key_total = k_ref.shape[0]
        slot = (lax.broadcasted_iota(jnp.int32, (1, key_total), 1) // chunk_rows) % LIST
        live = slot < count_ref[0]
        pieces = [
            one_group(live, q_ref, do_ref, k_ref, v_ref, o_ref, dq_ref, within)
            for within in range(groups_per_step)
        ]
        step = pl.program_id(0)
        for index in range(local_groups // groups_per_step):

            @pl.when(step == index)
            def _():
                for within, (key_piece, value_piece) in enumerate(pieces):
                    group = index * groups_per_step + within
                    key_cols = slice(group * HEAD_SIZE, (group + 1) * HEAD_SIZE)
                    value_cols = slice(
                        (local_groups + group) * HEAD_SIZE, (local_groups + group + 1) * HEAD_SIZE
                    )
                    pieces_ref[:, key_cols] = key_piece
                    pieces_ref[:, value_cols] = value_piece

    return kernel


def attend_all(queries, output_gradient, fetched, count, chunk_rows, groups_per_step=GROUPS_PER_STEP):
    query_rows, query_width = queries.shape
    key_total, both_width = fetched.shape
    key_width = both_width // 2
    local_groups = key_width // HEAD_SIZE
    groups_per_step = min(groups_per_step, local_groups)
    steps = local_groups // groups_per_step
    heads_per_group = QUERY_HEADS // KEY_VALUE_HEADS
    step_width = groups_per_step * heads_per_group * HEAD_SIZE
    key_step = groups_per_step * HEAD_SIZE
    row_block = pl.BlockSpec((query_rows, step_width), lambda i: (0, i))
    key_block = pl.BlockSpec((key_total, key_step), lambda i: (0, i))
    value_block = pl.BlockSpec((key_total, key_step), lambda i: (0, steps + i))
    return pl.pallas_call(
        attention_kernel(chunk_rows, heads_per_group, local_groups, groups_per_step),
        grid=(steps,),
        in_specs=[
            pl.BlockSpec(memory_space=pltpu.SMEM),
            row_block,
            row_block,
            key_block,
            value_block,
        ],
        out_specs=[row_block, row_block, pl.BlockSpec((key_total, both_width), lambda i: (0, 0))],
        out_shape=[
            jax.ShapeDtypeStruct((query_rows, query_width), jnp.bfloat16),
            jax.ShapeDtypeStruct((query_rows, query_width), jnp.bfloat16),
            jax.ShapeDtypeStruct((key_total, both_width), jnp.bfloat16),
        ],
    )(count, queries, output_gradient, fetched, fetched)


def make_shards(peers):
    def shards(
        queries, episode_key_cache, episode_value_cache, output_gradient, block_lists, block_counts
    ):
        row_count = episode_key_cache.shape[0]
        key_width = episode_key_cache.shape[2]
        both_width = 2 * key_width
        chunk_rows = row_count // peers

        held = jnp.concatenate(
            [episode_key_cache[:, 0, :], episode_value_cache[:, 0, :]], axis=1
        )
        first_send, listed, counted = lax.optimization_barrier(
            (jnp.pad(held, ((0, 0), (0, TAG_COLUMNS))), block_lists, block_counts)
        )
        tag = jnp.concatenate([listed[0], counted]).astype(jnp.bfloat16)
        tag_block = jnp.broadcast_to(
            jnp.pad(tag, (0, TAG_COLUMNS - LIST - 1)), (row_count, TAG_COLUMNS)
        )
        first_send = lax.dynamic_update_slice(first_send, tag_block, (0, both_width)).reshape(
            peers, chunk_rows, both_width + TAG_COLUMNS
        )
        first_recv = lax.all_to_all(first_send, "ctx", 0, 0, tiled=True)
        info = first_recv[:, 0, both_width : both_width + LIST + 1].astype(jnp.int32)
        lists_all = info[:, :LIST]
        counts_all = info[:, LIST]

        rows_held = first_recv[:, :, :both_width]
        picked = jnp.take(rows_held, lists_all, axis=0, mode="clip").reshape(
            peers, LIST * chunk_rows, both_width
        )
        slot_live = jnp.arange(LIST, dtype=jnp.int32)[None, :] < counts_all[:, None]
        selector = (
            (lists_all[:, :, None] == jnp.arange(peers, dtype=jnp.int32)[None, None, :])
            & slot_live[:, :, None]
        ).astype(jnp.bfloat16)
        picked, selector = lax.optimization_barrier((picked, selector))
        fetched = lax.all_to_all(picked, "ctx", 0, 0, tiled=True).reshape(
            LIST * row_count, both_width
        )
        attn_out, query_grad, pieces = attend_all(
            queries,
            output_gradient,
            fetched,
            block_counts,
            chunk_rows,
        )

        pieces, selector = lax.optimization_barrier((pieces, selector))
        back = lax.all_to_all(
            pieces.reshape(peers, LIST * chunk_rows, both_width), "ctx", 0, 0, tiled=True
        ).reshape(peers, LIST, chunk_rows, both_width)
        summed = jnp.einsum(
            "qjrc,qjn->nrc", back, selector, preferred_element_type=jnp.float32
        ).astype(jnp.bfloat16)

        owned = lax.all_to_all(summed, "ctx", 0, 0, tiled=True).reshape(row_count, both_width)
        key_cache_gradient = owned[:, None, :key_width]
        value_cache_gradient = owned[:, None, key_width:]
        return attn_out, query_grad, key_cache_gradient, value_cache_gradient

    return shards


def solution(mesh):
    placed = (
        P(("parts", "ctx"), "tp"),
        P(None, ("parts", "ctx"), "tp"),
        P(None, ("parts", "ctx"), "tp"),
        P(("parts", "ctx"), "tp"),
        P(("parts", "ctx"), None),
        P(("parts", "ctx")),
    )
    return jax.shard_map(
        make_shards(mesh.shape["ctx"]),
        mesh=mesh,
        in_specs=placed,
        out_specs=(
            P(("parts", "ctx"), "tp"),
            P(("parts", "ctx"), "tp"),
            P(None, ("parts", "ctx"), "tp"),
            P(None, ("parts", "ctx"), "tp"),
        ),
        check_vma=False,
    )
```

```python
import jax
import jax.numpy as jnp
from jax import lax
from jax.experimental import pallas as pl
from jax.experimental.pallas import tpu as pltpu
from jax.sharding import PartitionSpec as P

QUERY_HEADS = 64
KEY_VALUE_HEADS = 8
HEAD_SIZE = 128
LIST = 2
TAG_COLUMNS = 128
GROUPS_PER_STEP = 4


def attention_kernel(chunk_rows, heads_per_group, local_groups, groups_per_step):
    score_scale = HEAD_SIZE ** (-0.5)
    group_width = heads_per_group * HEAD_SIZE

    def one_group(live, q_ref, do_ref, k_ref, v_ref, o_ref, dq_ref, within):
        key_cols = slice(within * HEAD_SIZE, (within + 1) * HEAD_SIZE)
        keys = k_ref[:, key_cols]
        values = v_ref[:, key_cols]
        query_rows = q_ref.shape[0]
        nt = (((1,), (1,)), ((), ()))
        tn = (((0,), (0,)), ((), ()))
        heads = [
            slice(within * group_width + a * HEAD_SIZE, within * group_width + (a + 1) * HEAD_SIZE)
            for a in range(heads_per_group)
        ]
        q = jnp.concatenate([q_ref[:, cols] for cols in heads], axis=0)
        do = jnp.concatenate([do_ref[:, cols] for cols in heads], axis=0)
        scores = score_scale * lax.dot_general(q, keys, nt, preferred_element_type=jnp.float32)
        masked = jnp.where(live, scores, -jnp.inf)
        peak = jnp.max(masked, axis=1, keepdims=True)
        exponent = jnp.exp(masked - peak)
        weights = exponent / jnp.sum(exponent, axis=1, keepdims=True)
        weights_low = weights.astype(jnp.bfloat16)
        attended = jnp.dot(weights_low, values, preferred_element_type=jnp.float32).astype(
            jnp.bfloat16
        )
        row_delta = jnp.sum(
            do.astype(jnp.float32) * attended.astype(jnp.float32), axis=1, keepdims=True
        )
        weight_grad = lax.dot_general(do, values, nt, preferred_element_type=jnp.float32)
        score_grad = (weights * (weight_grad - row_delta)).astype(jnp.bfloat16)
        query_grad = (
            score_scale * jnp.dot(score_grad, keys, preferred_element_type=jnp.float32)
        ).astype(jnp.bfloat16)
        for a, cols in enumerate(heads):
            o_ref[:, cols] = attended[a * query_rows : (a + 1) * query_rows]
            dq_ref[:, cols] = query_grad[a * query_rows : (a + 1) * query_rows]
        key_piece = (
            score_scale * lax.dot_general(score_grad, q, tn, preferred_element_type=jnp.float32)
        ).astype(jnp.bfloat16)
        value_piece = lax.dot_general(
            weights_low, do, tn, preferred_element_type=jnp.float32
        ).astype(jnp.bfloat16)
        return key_piece, value_piece

    def kernel(count_ref, q_ref, do_ref, k_ref, v_ref, o_ref, dq_ref, pieces_ref):
        key_total = k_ref.shape[0]
        slot = (lax.broadcasted_iota(jnp.int32, (1, key_total), 1) // chunk_rows) % LIST
        live = slot < count_ref[0]
        pieces = [
            one_group(live, q_ref, do_ref, k_ref, v_ref, o_ref, dq_ref, within)
            for within in range(groups_per_step)
        ]
        step = pl.program_id(0)
        for index in range(local_groups // groups_per_step):

            @pl.when(step == index)
            def _():
                for within, (key_piece, value_piece) in enumerate(pieces):
                    group = index * groups_per_step + within
                    key_cols = slice(group * HEAD_SIZE, (group + 1) * HEAD_SIZE)
                    value_cols = slice(
                        (local_groups + group) * HEAD_SIZE, (local_groups + group + 1) * HEAD_SIZE
                    )
                    pieces_ref[:, key_cols] = key_piece
                    pieces_ref[:, value_cols] = value_piece

    return kernel


def attend_all(queries, output_gradient, fetched, count, chunk_rows, groups_per_step=GROUPS_PER_STEP):
    query_rows, query_width = queries.shape
    key_total, both_width = fetched.shape
    key_width = both_width // 2
    local_groups = key_width // HEAD_SIZE
    groups_per_step = min(groups_per_step, local_groups)
    steps = local_groups // groups_per_step
    heads_per_group = QUERY_HEADS // KEY_VALUE_HEADS
    step_width = groups_per_step * heads_per_group * HEAD_SIZE
    key_step = groups_per_step * HEAD_SIZE
    row_block = pl.BlockSpec((query_rows, step_width), lambda i: (0, i))
    key_block = pl.BlockSpec((key_total, key_step), lambda i: (0, i))
    value_block = pl.BlockSpec((key_total, key_step), lambda i: (0, steps + i))
    return pl.pallas_call(
        attention_kernel(chunk_rows, heads_per_group, local_groups, groups_per_step),
        grid=(steps,),
        in_specs=[
            pl.BlockSpec(memory_space=pltpu.SMEM),
            row_block,
            row_block,
            key_block,
            value_block,
        ],
        out_specs=[row_block, row_block, pl.BlockSpec((key_total, both_width), lambda i: (0, 0))],
        out_shape=[
            jax.ShapeDtypeStruct((query_rows, query_width), jnp.bfloat16),
            jax.ShapeDtypeStruct((query_rows, query_width), jnp.bfloat16),
            jax.ShapeDtypeStruct((key_total, both_width), jnp.bfloat16),
        ],
    )(count, queries, output_gradient, fetched, fetched)


def make_shards(peers):
    def shards(
        queries, episode_key_cache, episode_value_cache, output_gradient, block_lists, block_counts
    ):
        row_count = episode_key_cache.shape[0]
        key_width = episode_key_cache.shape[2]
        both_width = 2 * key_width
        chunk_rows = row_count // peers

        held = jnp.concatenate(
            [episode_key_cache[:, 0, :], episode_value_cache[:, 0, :]], axis=1
        )
        first_send, listed, counted = lax.optimization_barrier(
            (jnp.pad(held, ((0, 0), (0, TAG_COLUMNS))), block_lists, block_counts)
        )
        tag = jnp.concatenate([listed[0], counted]).astype(jnp.bfloat16)
        tag_block = jnp.broadcast_to(
            jnp.pad(tag, (0, TAG_COLUMNS - LIST - 1)), (row_count, TAG_COLUMNS)
        )
        first_send = lax.dynamic_update_slice(first_send, tag_block, (0, both_width)).reshape(
            peers, chunk_rows, both_width + TAG_COLUMNS
        )
        first_recv = lax.all_to_all(first_send, "ctx", 0, 0, tiled=True)
        info = first_recv[:, 0, both_width:].astype(jnp.int32)
        lists_all = info[:, :LIST]
        counts_all = info[:, LIST]

        rows_held = first_recv[:, :, :both_width]
        picked = jnp.take(rows_held, lists_all, axis=0, mode="clip").reshape(
            peers, LIST * chunk_rows, both_width
        )
        slot_live = jnp.arange(LIST, dtype=jnp.int32)[None, :] < counts_all[:, None]
        selector = (
            (lists_all[:, :, None] == jnp.arange(peers, dtype=jnp.int32)[None, None, :])
            & slot_live[:, :, None]
        ).astype(jnp.bfloat16)
        picked, selector = lax.optimization_barrier((picked, selector))
        fetched = lax.all_to_all(picked, "ctx", 0, 0, tiled=True).reshape(
            LIST * row_count, both_width
        )
        attn_out, query_grad, pieces = attend_all(
            queries,
            output_gradient,
            fetched,
            block_counts,
            chunk_rows,
        )

        pieces, selector = lax.optimization_barrier((pieces, selector))
        back = lax.all_to_all(
            pieces.reshape(peers, LIST * chunk_rows, both_width), "ctx", 0, 0, tiled=True
        ).reshape(peers, LIST, chunk_rows, both_width)
        summed = jnp.einsum(
            "qjrc,qjn->nrc", back, selector, preferred_element_type=jnp.float32
        ).astype(jnp.bfloat16)

        owned = lax.all_to_all(summed, "ctx", 0, 0, tiled=True).reshape(row_count, both_width)
        key_cache_gradient = owned[:, None, :key_width]
        value_cache_gradient = owned[:, None, key_width:]
        return attn_out, query_grad, key_cache_gradient, value_cache_gradient

    return shards


def solution(mesh):
    placed = (
        P(("parts", "ctx"), "tp"),
        P(None, ("parts", "ctx"), "tp"),
        P(None, ("parts", "ctx"), "tp"),
        P(("parts", "ctx"), "tp"),
        P(("parts", "ctx"), None),
        P(("parts", "ctx")),
    )
    return jax.shard_map(
        make_shards(mesh.shape["ctx"]),
        mesh=mesh,
        in_specs=placed,
        out_specs=(
            P(("parts", "ctx"), "tp"),
            P(("parts", "ctx"), "tp"),
            P(None, ("parts", "ctx"), "tp"),
            P(None, ("parts", "ctx"), "tp"),
        ),
        check_vma=False,
    )
```

```python
import jax
import jax.numpy as jnp
from jax import lax
from jax.experimental import pallas as pl
from jax.experimental.pallas import tpu as pltpu
from jax.sharding import PartitionSpec as P

QUERY_HEADS = 64
KEY_VALUE_HEADS = 8
HEAD_SIZE = 128
LIST = 2
TAG_COLUMNS = 128
GROUPS_PER_STEP = 4


def attention_kernel(chunk_rows, heads_per_group, local_groups, groups_per_step):
    score_scale = HEAD_SIZE ** (-0.5)
    group_width = heads_per_group * HEAD_SIZE

    def one_group(live, q_ref, do_ref, k_ref, v_ref, o_ref, dq_ref, within):
        key_cols = slice(within * HEAD_SIZE, (within + 1) * HEAD_SIZE)
        keys = k_ref[:, key_cols]
        values = v_ref[:, key_cols]
        query_rows = q_ref.shape[0]
        nt = (((1,), (1,)), ((), ()))
        heads = [
            slice(within * group_width + a * HEAD_SIZE, within * group_width + (a + 1) * HEAD_SIZE)
            for a in range(heads_per_group)
        ]
        q = jnp.concatenate([q_ref[:, cols] for cols in heads], axis=0)
        do = jnp.concatenate([do_ref[:, cols] for cols in heads], axis=0)
        scores = score_scale * lax.dot_general(q, keys, nt, preferred_element_type=jnp.float32)
        masked = jnp.where(live, scores, -jnp.inf)
        peak = jnp.max(masked, axis=1, keepdims=True)
        exponent = jnp.exp(masked - peak)
        weights = exponent / jnp.sum(exponent, axis=1, keepdims=True)
        weights_low = weights.astype(jnp.bfloat16)
        attended = jnp.dot(weights_low, values, preferred_element_type=jnp.float32).astype(
            jnp.bfloat16
        )
        row_delta = jnp.sum(
            do.astype(jnp.float32) * attended.astype(jnp.float32), axis=1, keepdims=True
        )
        weight_grad = lax.dot_general(do, values, nt, preferred_element_type=jnp.float32)
        score_grad = (weights * (weight_grad - row_delta)).astype(jnp.bfloat16)
        query_grad = (
            score_scale * jnp.dot(score_grad, keys, preferred_element_type=jnp.float32)
        ).astype(jnp.bfloat16)
        for a, cols in enumerate(heads):
            o_ref[:, cols] = attended[a * query_rows : (a + 1) * query_rows]
            dq_ref[:, cols] = query_grad[a * query_rows : (a + 1) * query_rows]
        key_piece = (
            score_scale * jnp.dot(q.T, score_grad, preferred_element_type=jnp.float32).T
        ).astype(jnp.bfloat16)
        value_piece = jnp.dot(do.T, weights_low, preferred_element_type=jnp.float32).T.astype(
            jnp.bfloat16
        )
        return key_piece, value_piece

    def kernel(count_ref, q_ref, do_ref, k_ref, v_ref, o_ref, dq_ref, pieces_ref):
        key_total = k_ref.shape[0]
        slot = (lax.broadcasted_iota(jnp.int32, (1, key_total), 1) // chunk_rows) % LIST
        live = slot < count_ref[0]
        pieces = [
            one_group(live, q_ref, do_ref, k_ref, v_ref, o_ref, dq_ref, within)
            for within in range(groups_per_step)
        ]
        step = pl.program_id(0)
        for index in range(local_groups // groups_per_step):

            @pl.when(step == index)
            def _():
                for within, (key_piece, value_piece) in enumerate(pieces):
                    group = index * groups_per_step + within
                    key_cols = slice(group * HEAD_SIZE, (group + 1) * HEAD_SIZE)
                    value_cols = slice(
                        (local_groups + group) * HEAD_SIZE, (local_groups + group + 1) * HEAD_SIZE
                    )
                    pieces_ref[:, key_cols] = key_piece
                    pieces_ref[:, value_cols] = value_piece

    return kernel


def attend_all(queries, output_gradient, fetched, count, chunk_rows, groups_per_step=GROUPS_PER_STEP):
    query_rows, query_width = queries.shape
    key_total, both_width = fetched.shape
    key_width = both_width // 2
    local_groups = key_width // HEAD_SIZE
    groups_per_step = min(groups_per_step, local_groups)
    steps = local_groups // groups_per_step
    heads_per_group = QUERY_HEADS // KEY_VALUE_HEADS
    step_width = groups_per_step * heads_per_group * HEAD_SIZE
    key_step = groups_per_step * HEAD_SIZE
    row_block = pl.BlockSpec((query_rows, step_width), lambda i: (0, i))
    key_block = pl.BlockSpec((key_total, key_step), lambda i: (0, i))
    value_block = pl.BlockSpec((key_total, key_step), lambda i: (0, steps + i))
    return pl.pallas_call(
        attention_kernel(chunk_rows, heads_per_group, local_groups, groups_per_step),
        grid=(steps,),
        in_specs=[
            pl.BlockSpec(memory_space=pltpu.SMEM),
            row_block,
            row_block,
            key_block,
            value_block,
        ],
        out_specs=[row_block, row_block, pl.BlockSpec((key_total, both_width), lambda i: (0, 0))],
        out_shape=[
            jax.ShapeDtypeStruct((query_rows, query_width), jnp.bfloat16),
            jax.ShapeDtypeStruct((query_rows, query_width), jnp.bfloat16),
            jax.ShapeDtypeStruct((key_total, both_width), jnp.bfloat16),
        ],
    )(count, queries, output_gradient, fetched, fetched)


def make_shards(peers):
    def shards(
        queries, episode_key_cache, episode_value_cache, output_gradient, block_lists, block_counts
    ):
        row_count = episode_key_cache.shape[0]
        key_width = episode_key_cache.shape[2]
        both_width = 2 * key_width
        chunk_rows = row_count // peers

        held = jnp.concatenate(
            [episode_key_cache[:, 0, :], episode_value_cache[:, 0, :]], axis=1
        )
        first_send, listed, counted = lax.optimization_barrier(
            (jnp.pad(held, ((0, 0), (0, TAG_COLUMNS))), block_lists, block_counts)
        )
        tag = jnp.concatenate([listed[0], counted]).astype(jnp.bfloat16)
        tag_block = jnp.broadcast_to(
            jnp.pad(tag, (0, TAG_COLUMNS - LIST - 1)), (row_count, TAG_COLUMNS)
        )
        first_send = lax.dynamic_update_slice(first_send, tag_block, (0, both_width)).reshape(
            peers, chunk_rows, both_width + TAG_COLUMNS
        )
        first_recv = lax.all_to_all(first_send, "ctx", 0, 0, tiled=True)
        info = first_recv[:, 0, both_width:].astype(jnp.int32)
        lists_all = info[:, :LIST]
        counts_all = info[:, LIST]

        rows_held = first_recv[:, :, :both_width]
        picked = jnp.take(rows_held, lists_all, axis=0, mode="clip").reshape(
            peers, LIST * chunk_rows, both_width
        )
        slot_live = jnp.arange(LIST, dtype=jnp.int32)[None, :] < counts_all[:, None]
        selector = (
            (lists_all[:, :, None] == jnp.arange(peers, dtype=jnp.int32)[None, None, :])
            & slot_live[:, :, None]
        ).astype(jnp.bfloat16)
        picked, selector = lax.optimization_barrier((picked, selector))
        fetched = lax.all_to_all(picked, "ctx", 0, 0, tiled=True).reshape(
            LIST * row_count, both_width
        )
        attn_out, query_grad, pieces = attend_all(
            queries,
            output_gradient,
            fetched,
            block_counts,
            chunk_rows,
        )

        pieces, selector = lax.optimization_barrier((pieces, selector))
        back = lax.all_to_all(
            pieces.reshape(peers, LIST * chunk_rows, both_width), "ctx", 0, 0, tiled=True
        ).reshape(peers, LIST, chunk_rows, both_width)
        summed = jnp.einsum(
            "qjn,qjrc->nrc", selector, back, preferred_element_type=jnp.float32
        ).astype(jnp.bfloat16)

        owned = lax.all_to_all(summed, "ctx", 0, 0, tiled=True).reshape(row_count, both_width)
        key_cache_gradient = owned[:, None, :key_width]
        value_cache_gradient = owned[:, None, key_width:]
        return attn_out, query_grad, key_cache_gradient, value_cache_gradient

    return shards


def solution(mesh):
    placed = (
        P(("parts", "ctx"), "tp"),
        P(None, ("parts", "ctx"), "tp"),
        P(None, ("parts", "ctx"), "tp"),
        P(("parts", "ctx"), "tp"),
        P(("parts", "ctx"), None),
        P(("parts", "ctx")),
    )
    return jax.shard_map(
        make_shards(mesh.shape["ctx"]),
        mesh=mesh,
        in_specs=placed,
        out_specs=(
            P(("parts", "ctx"), "tp"),
            P(("parts", "ctx"), "tp"),
            P(None, ("parts", "ctx"), "tp"),
            P(None, ("parts", "ctx"), "tp"),
        ),
        check_vma=False,
    )
```

```python
import jax
import jax.numpy as jnp
from jax import lax
from jax.experimental import pallas as pl
from jax.experimental.pallas import tpu as pltpu
from jax.sharding import PartitionSpec as P

QUERY_HEADS = 64
KEY_VALUE_HEADS = 8
HEAD_SIZE = 128
LIST = 2
TAG_COLUMNS = 128
GROUPS_PER_STEP = 4


def attention_kernel(chunk_rows, heads_per_group, local_groups, groups_per_step):
    score_scale = HEAD_SIZE ** (-0.5)
    group_width = heads_per_group * HEAD_SIZE

    def one_group(live, q_ref, do_ref, k_ref, v_ref, o_ref, dq_ref, within):
        key_cols = slice(within * HEAD_SIZE, (within + 1) * HEAD_SIZE)
        keys = k_ref[:, key_cols]
        values = v_ref[:, key_cols]
        query_rows = q_ref.shape[0]
        nt = (((1,), (1,)), ((), ()))
        heads = [
            slice(within * group_width + a * HEAD_SIZE, within * group_width + (a + 1) * HEAD_SIZE)
            for a in range(heads_per_group)
        ]
        q = jnp.concatenate([q_ref[:, cols] for cols in heads], axis=0)
        do = jnp.concatenate([do_ref[:, cols] for cols in heads], axis=0)
        scores = score_scale * lax.dot_general(q, keys, nt, preferred_element_type=jnp.float32)
        masked = jnp.where(live, scores, -jnp.inf)
        peak = jnp.max(masked, axis=1, keepdims=True)
        exponent = jnp.exp(masked - peak)
        weights = exponent / jnp.sum(exponent, axis=1, keepdims=True)
        weights_low = weights.astype(jnp.bfloat16)
        attended = jnp.dot(weights_low, values, preferred_element_type=jnp.float32).astype(
            jnp.bfloat16
        )
        row_delta = jnp.sum(
            do.astype(jnp.float32) * attended.astype(jnp.float32), axis=1, keepdims=True
        )
        weight_grad = lax.dot_general(do, values, nt, preferred_element_type=jnp.float32)
        score_grad = (weights * (weight_grad - row_delta)).astype(jnp.bfloat16)
        query_grad = (
            score_scale * jnp.dot(score_grad, keys, preferred_element_type=jnp.float32)
        ).astype(jnp.bfloat16)
        for a, cols in enumerate(heads):
            o_ref[:, cols] = attended[a * query_rows : (a + 1) * query_rows]
            dq_ref[:, cols] = query_grad[a * query_rows : (a + 1) * query_rows]
        key_piece = (
            score_scale * jnp.dot(q.T, score_grad, preferred_element_type=jnp.float32).T
        ).astype(jnp.bfloat16)
        value_piece = jnp.dot(do.T, weights_low, preferred_element_type=jnp.float32).T.astype(
            jnp.bfloat16
        )
        return key_piece, value_piece

    def kernel(count_ref, q_ref, do_ref, k_ref, v_ref, o_ref, dq_ref, pieces_ref):
        key_total = k_ref.shape[0]
        slot = (lax.broadcasted_iota(jnp.int32, (1, key_total), 1) // chunk_rows) % LIST
        live = slot < count_ref[0]
        pieces = [
            one_group(live, q_ref, do_ref, k_ref, v_ref, o_ref, dq_ref, within)
            for within in range(groups_per_step)
        ]
        step = pl.program_id(0)
        for index in range(local_groups // groups_per_step):

            @pl.when(step == index)
            def _():
                for within, (key_piece, value_piece) in enumerate(pieces):
                    group = index * groups_per_step + within
                    key_cols = slice(group * HEAD_SIZE, (group + 1) * HEAD_SIZE)
                    value_cols = slice(
                        (local_groups + group) * HEAD_SIZE, (local_groups + group + 1) * HEAD_SIZE
                    )
                    pieces_ref[:, key_cols] = key_piece
                    pieces_ref[:, value_cols] = value_piece

    return kernel


def attend_all(queries, output_gradient, fetched, count, chunk_rows, groups_per_step=GROUPS_PER_STEP):
    query_rows, query_width = queries.shape
    key_total, both_width = fetched.shape
    key_width = both_width // 2
    local_groups = key_width // HEAD_SIZE
    groups_per_step = min(groups_per_step, local_groups)
    steps = local_groups // groups_per_step
    heads_per_group = QUERY_HEADS // KEY_VALUE_HEADS
    step_width = groups_per_step * heads_per_group * HEAD_SIZE
    key_step = groups_per_step * HEAD_SIZE
    row_block = pl.BlockSpec((query_rows, step_width), lambda i: (0, i))
    key_block = pl.BlockSpec((key_total, key_step), lambda i: (0, i))
    value_block = pl.BlockSpec((key_total, key_step), lambda i: (0, steps + i))
    return pl.pallas_call(
        attention_kernel(chunk_rows, heads_per_group, local_groups, groups_per_step),
        grid=(steps,),
        in_specs=[
            pl.BlockSpec(memory_space=pltpu.SMEM),
            row_block,
            row_block,
            key_block,
            value_block,
        ],
        out_specs=[row_block, row_block, pl.BlockSpec((key_total, both_width), lambda i: (0, 0))],
        out_shape=[
            jax.ShapeDtypeStruct((query_rows, query_width), jnp.bfloat16),
            jax.ShapeDtypeStruct((query_rows, query_width), jnp.bfloat16),
            jax.ShapeDtypeStruct((key_total, both_width), jnp.bfloat16),
        ],
    )(count, queries, output_gradient, fetched, fetched)


def make_shards(peers):
    def shards(
        queries, episode_key_cache, episode_value_cache, output_gradient, block_lists, block_counts
    ):
        row_count = episode_key_cache.shape[0]
        key_width = episode_key_cache.shape[2]
        both_width = 2 * key_width
        chunk_rows = row_count // peers

        held = jnp.concatenate(
            [episode_key_cache[:, 0, :], episode_value_cache[:, 0, :]], axis=1
        )
        first_send, listed, counted = lax.optimization_barrier(
            (jnp.pad(held, ((0, 0), (0, TAG_COLUMNS))), block_lists, block_counts)
        )
        tag = jnp.concatenate([listed[0], counted]).astype(jnp.bfloat16)
        tag_block = jnp.broadcast_to(
            jnp.pad(tag, (0, TAG_COLUMNS - LIST - 1)), (row_count, TAG_COLUMNS)
        )
        first_send = lax.dynamic_update_slice(first_send, tag_block, (0, both_width)).reshape(
            peers, chunk_rows, both_width + TAG_COLUMNS
        )
        first_recv = lax.all_to_all(first_send, "ctx", 0, 0, tiled=True)
        info = first_recv[:, 0, both_width:].astype(jnp.int32)
        lists_all = info[:, :LIST]
        counts_all = info[:, LIST]

        rows_held = first_recv[:, :, :both_width]
        picked = jnp.take(rows_held, lists_all, axis=0, mode="clip").reshape(
            peers, LIST * chunk_rows, both_width
        )
        slot_live = jnp.arange(LIST, dtype=jnp.int32)[None, :] < counts_all[:, None]
        selector = (
            (lists_all[:, :, None] == jnp.arange(peers, dtype=jnp.int32)[None, None, :])
            & slot_live[:, :, None]
        ).astype(jnp.bfloat16)
        picked, selector = lax.optimization_barrier((picked, selector))
        fetched = lax.all_to_all(picked, "ctx", 0, 0, tiled=True).reshape(
            LIST * row_count, both_width
        )
        attn_out, query_grad, pieces = attend_all(
            queries,
            output_gradient,
            fetched,
            block_counts,
            chunk_rows,
        )

        pieces, selector = lax.optimization_barrier((pieces, selector))
        back = lax.all_to_all(
            pieces.reshape(peers, LIST * chunk_rows, both_width), "ctx", 0, 0, tiled=True
        ).reshape(peers, LIST, chunk_rows, both_width)
        summed = jnp.sum(
            back.astype(jnp.float32)[None] * selector.astype(jnp.float32).transpose(2, 0, 1)[:, :, :, None, None],
            axis=(1, 2),
        ).astype(jnp.bfloat16)

        owned = lax.all_to_all(summed, "ctx", 0, 0, tiled=True).reshape(row_count, both_width)
        key_cache_gradient = owned[:, None, :key_width]
        value_cache_gradient = owned[:, None, key_width:]
        return attn_out, query_grad, key_cache_gradient, value_cache_gradient

    return shards


def solution(mesh):
    placed = (
        P(("parts", "ctx"), "tp"),
        P(None, ("parts", "ctx"), "tp"),
        P(None, ("parts", "ctx"), "tp"),
        P(("parts", "ctx"), "tp"),
        P(("parts", "ctx"), None),
        P(("parts", "ctx")),
    )
    return jax.shard_map(
        make_shards(mesh.shape["ctx"]),
        mesh=mesh,
        in_specs=placed,
        out_specs=(
            P(("parts", "ctx"), "tp"),
            P(("parts", "ctx"), "tp"),
            P(None, ("parts", "ctx"), "tp"),
            P(None, ("parts", "ctx"), "tp"),
        ),
        check_vma=False,
    )
```
